512 devices in a mesh: ctx: 64 (over z, y), chan: 4 (over x), phase: 2 (over core).
Axes of the slice: x: 4, y: 8, z: 8, core: 2. Of those that a mesh axis runs over, the one named last changes fastest.
Arguments:
- projected: bfloat16 [2, 3, 16384, 8192], P('phase', None, 'ctx', 'chan'), may hold values from -6 to 6
- short_filter: float32 [2, 3, 3, 8192], P('phase', None, None, 'chan'), may hold values from -3.5 to 3.5
- decay_rate: float32 [2, 64, 16], P('phase', 'chan'), may hold values from 1.8310547e-05 to 0.08, as said below
- residue: float32 [2, 64, 16], P('phase', 'chan'), may hold values from -0.25980762 to 0.25980762
- norm_gain: float32 [2, 8192], P('phase', 'chan'), may hold values from 0.1 to 1.9
- lengths: int32 [2, 4], P('phase'), may hold values from 1 to 6144, 16384 in all within a row
Outputs:
- handoff: bfloat16 [2, 16384, 8192], P('phase', 'ctx', 'chan')
The draws below stay inside these ranges and needn't reach their ends.
Inputs may be any that keep to these rules, and one draw needn't show every extreme that they name: Each row holds 4 sequence lengths, two preference pairs (chosen, then rejected), that sum to 16384; the longest is exactly 6144. `decay_rate`: positive decay rates.
All inputs are finite; a program needn't handle non-finite values.
Results may differ from the reference program's by a relative error of at most 0.0061.
Values may be sent and summed in bfloat16 or wider, within the bound.
No kernel may reach another device: no remote copies, remote signals or barrier semaphores. Data moves between devices by JAX's collectives and lax.ppermute only.
A program may use at most 64 MiB of HBM per device.

```python
import math
import jax
import jax.numpy as jnp
import numpy as np
from jax import lax

D = 8192
GW = 128
GROUPS = 64
MODES = 16
SHORT = 3
TOK_DEV = 256
TOKENS = 16384
NSEQ = 4
LONGEST = 6144
N_CTX = 64


def modal_pair(key):
    base_key = jax.random.fold_in(key, 17)
    first_key, second_key = jax.random.split(base_key)
    spread = jax.random.uniform(first_key, (2, GROUPS, MODES), jnp.float32)
    lowest = math.log(0.3 / TOKENS)
    highest = math.log(0.08)
    pole_rate = jnp.exp(lowest + (highest - lowest) * spread)
    grade = 1.0 + 2.0 * jnp.arange(GROUPS, dtype=jnp.float32) / max(GROUPS - 1, 1)
    amplitude = jax.random.uniform(second_key, (2, GROUPS, MODES), jnp.float32, minval=-1.5, maxval=1.5)
    residue_vals = amplitude * jnp.sqrt(2.0 * pole_rate / MODES) * jnp.sqrt(grade)[None, :, None]
    return (pole_rate, residue_vals)


def draw_decay_rate(key, part):
    return modal_pair(key)[0]


def draw_residue(key, part):
    return modal_pair(key)[1]


def steps_of(stream_key, shape, cuts, low, top_value):
    def one(position, blocks):
        draws = jax.random.uniform(jax.random.fold_in(jax.random.fold_in(stream_key, 6), position), (blocks,), jnp.float32, low / len(cuts), top_value / len(cuts))
        return jnp.repeat(jnp.exp(draws), shape[position] // blocks).reshape((-1,) + (1,) * (len(shape) - position - 1))

    level = one(*cuts[0])
    for cut in cuts[1:]:
        level = level * one(*cut)
    return level


def profile(count, total, limit, lean):
    portions = [(1 << 20) // math.isqrt(standing ** lean) + 1 for standing in range(2, count + 1)]
    rest, holding = total - limit - (count - 1), [1] * (count - 1)
    while rest > 0:
        candidates = [i for i in range(count - 1) if holding[i] < limit]
        pool, remaining = sum([portions[i] for i in candidates]), rest
        for i in candidates:
            extra = min(limit - holding[i], max(1, remaining * portions[i] // pool), rest)
            holding[i] = holding[i] + extra
            rest = rest - extra
    return np.array([limit] + holding)


def ragged_sizes(key, amount, total, reach, skew):
    if amount == 2:
        one = jax.random.randint(key, (), max(1, total - reach), min(reach, total - 1) + 1)
        return jnp.stack([one, total - one])
    sizes = jnp.asarray(profile(amount, total, reach, skew), jnp.int32)
    couples = (amount - 1) // 2
    donor, receiver = sizes[1:1 + 2 * couples:2], sizes[2:2 + 2 * couples:2]
    room = jnp.minimum(donor - 1, reach - receiver)
    passed = jax.random.randint(jax.random.fold_in(key, 1), (couples,), 0, 1 << 20) % (room + 1)
    sizes = sizes.at[1:1 + 2 * couples:2].set(donor - passed).at[2:2 + 2 * couples:2].set(receiver + passed)
    return sizes[jax.random.permutation(jax.random.fold_in(key, 2), amount)]


def normal_values(key, extent, scale, reach, shards=(), kind=jnp.bfloat16):
    loudness = steps_of(key, extent, shards, -0.22, 0.18) if shards else 1.0
    array = jax.random.normal(key, extent, jnp.float32) * scale * loudness
    return jnp.minimum(jnp.maximum(array, -reach), reach).astype(kind)


def setup_inputs(seed: int = 0) -> dict:
    key_of = jax.random.split(jax.random.key(seed), 7)
    projected = normal_values(key_of[0], (2, 3, TOKENS, D), 1.0, 6.0, ((0, 2), (2, 64), (3, 4)))
    short_filter = normal_values(key_of[1], (2, 3, SHORT, D), SHORT ** -0.5, 3.5, ((0, 2), (3, 4)), jnp.float32)
    decay_rate = draw_decay_rate(jax.random.fold_in(key_of[6], 71), 0)
    residue = draw_residue(jax.random.fold_in(key_of[6], 71), 0)
    norm_gain = jnp.clip(1.0 + 0.18 * jax.random.normal(key_of[4], (2, D), jnp.float32), 0.1, 1.9)
    lengths = jax.vmap(lambda own: ragged_sizes(own, NSEQ, TOKENS, LONGEST, 2))(jax.random.split(key_of[5], 2)).reshape((2, NSEQ)).astype(jnp.int32)
    return {"projected": projected, "short_filter": short_filter, "decay_rate": decay_rate, "residue": residue, "norm_gain": norm_gain, "lengths": lengths}


EPSILON = 1e-05

def segment_starts(seq_lengths, positions):
    starts = jnp.cumsum(seq_lengths) - seq_lengths
    chosen = jnp.where(starts[None, :] <= positions[:, None], starts[None, :], 0)
    return lax.optimization_barrier(jnp.max(chosen, axis=1)).astype(jnp.int32)

def lag_kernel(pole_rate, residue_here, block_len):
    row_index = jnp.arange(block_len, dtype=jnp.int32)
    lag_steps = row_index[:, None] - row_index[None, :]
    causal = lag_steps >= 0
    lag_float = jnp.maximum(lag_steps, 0).astype(pole_rate.dtype)
    summed = jnp.zeros((pole_rate.shape[0], block_len, block_len), pole_rate.dtype)
    for mode_index in range(pole_rate.shape[1]):
        summed = summed + residue_here[:, mode_index, None, None] * jnp.exp(-pole_rate[:, mode_index, None, None] * lag_float[None])
    return jnp.where(causal[None], summed, 0.0).astype(jnp.bfloat16)

def short_conv(features, filters, starts):
    length = features.shape[1]
    positions = jnp.arange(length, dtype=jnp.int32)
    padded = jnp.concatenate([jnp.zeros((3, SHORT - 1, features.shape[2]), jnp.bfloat16), features], axis=1)
    summed = jnp.zeros((3, length, features.shape[2]), filters.dtype)
    for tap_index in range(SHORT):
        shifted = padded[:, SHORT - 1 - tap_index:SHORT - 1 - tap_index + length]
        usable = (positions - tap_index >= starts).astype(filters.dtype)
        summed = summed + filters[:, tap_index, None, :] * shifted.astype(filters.dtype) * usable[None, :, None]
    return summed

def long_conv(gated_prod, pole_rate, residue_here, starts):
    float_kind = pole_rate.dtype
    block_len = TOK_DEV
    groups = pole_rate.shape[0]
    kernel = lag_kernel(pole_rate, residue_here, block_len)
    within = jnp.arange(block_len, dtype=jnp.int32)
    gated_blocks = gated_prod.reshape(N_CTX, block_len, groups, GW)
    start_blocks = starts.reshape(N_CTX, block_len)
    highest = lax.Precision.HIGHEST

    def advance(state, inputs):
        block_vals, block_starts, block_index = inputs
        anchor = block_index * block_len
        global_pos = anchor + within
        inside = (within[None, :] <= within[:, None]) & (global_pos[None, :] >= block_starts[:, None])
        masked = jnp.where(inside[None], kernel, jnp.zeros((), jnp.bfloat16)).astype(float_kind)
        values = block_vals.astype(float_kind)
        intra_term = jnp.einsum('gts,sgc->tgc', masked, values, precision=highest)
        carry_rows = (block_starts < anchor).astype(float_kind)
        reaching = residue_here[None] * jnp.exp(-pole_rate[None] * (within[:, None, None] + 1).astype(float_kind)) * carry_rows[:, None, None]
        inter_term = jnp.einsum('tgm,gmc->tgc', reaching, state, precision=highest)
        last_start = block_starts[block_len - 1]
        kept_rows = (global_pos >= last_start).astype(float_kind)
        fading = jnp.exp(-pole_rate[None] * (block_len - 1 - within)[:, None, None].astype(float_kind)) * kept_rows[:, None, None]
        fresh_state = jnp.einsum('sgm,sgc->gmc', fading, values, precision=highest)
        through = jnp.where(last_start < anchor, jnp.exp(-pole_rate * block_len), 0.0)
        new_state = through[:, :, None] * state + fresh_state
        return (new_state, (intra_term + inter_term).astype(jnp.bfloat16))
    initial = jnp.zeros((groups, pole_rate.shape[1], GW), float_kind)
    _, block_outs = lax.scan(advance, initial, (gated_blocks, start_blocks, jnp.arange(N_CTX, dtype=jnp.int32)))
    return block_outs.reshape(TOKENS, D)

def section(features, filters, pole_rate, residue_here, gain_row, seq_lengths):
    positions = jnp.arange(TOKENS, dtype=jnp.int32)
    starts = segment_starts(seq_lengths, positions)
    short_out = short_conv(features, filters, starts)
    gated_prod = (short_out[1] * short_out[2]).astype(jnp.bfloat16)
    mixed_conv = long_conv(gated_prod, pole_rate, residue_here, starts)
    activity = short_out[0] * mixed_conv.astype(short_out.dtype)
    squares = lax.optimization_barrier(jnp.sum(activity * activity, axis=1, keepdims=True))
    return (activity * lax.rsqrt(squares / D + EPSILON) * gain_row[None, :]).astype(jnp.bfloat16)

def reference(projected, short_filter, decay_rate, residue, norm_gain, lengths):
    first_out = section(projected[0], short_filter[0], decay_rate[0], residue[0], norm_gain[0], lengths[0])
    second_out = section(projected[1], short_filter[1], decay_rate[1], residue[1], norm_gain[1], lengths[1])
    return jnp.stack([second_out, first_out])
```

```python
import jax
import jax.numpy as jnp
from jax import lax
from jax.sharding import PartitionSpec as P

GW = 128
SHORT = 3
LONGEST = 6144

EPSILON = 1e-05
HIGHEST = lax.Precision.HIGHEST


def from_behind(shard, axis, by):
    length = lax.axis_size(axis)
    pairs = [(i, i + by) for i in range(length) if 0 <= i + by < length]
    return lax.ppermute(shard, axis, pairs)


def from_behind_2(value, axis, steps):
    count = lax.axis_size(axis)
    pairs = [(source, (source + steps) % count) for source in range(count)]
    return lax.ppermute(value, axis, pairs)


def butterfly_sum(value, axis):
    count = lax.axis_size(axis)
    step = 1
    while step < count:
        pairs = [(i, i ^ step) for i in range(count)]
        value = value + lax.ppermute(value, axis, pairs)
        step *= 2
    return value


def segment_starts(seq_lengths, positions):
    starts = jnp.cumsum(seq_lengths) - seq_lengths
    chosen = jnp.where(starts[None, :] <= positions[:, None], starts[None, :], 0)
    return jnp.max(chosen, axis=1)


def prior_states(through, fresh, block_len):
    ctx_count = lax.axis_size("ctx")
    need = min(ctx_count, LONGEST // block_len + 1)
    decay = from_behind(through, "ctx", 1)
    state = from_behind(fresh, "ctx", 1)
    cover = 1
    while cover < need:
        decay_before = from_behind(decay, "ctx", cover)
        state_before = from_behind(state, "ctx", cover)
        state = decay[..., None] * state_before + state
        decay = decay * decay_before
        cover *= 2
    return state


def on_device(projected, short_filter, decay_rate, residue, norm_gain, lengths):
    features = projected[0]
    filters = short_filter[0]
    pole_rate = decay_rate[0]
    residue_here = residue[0]
    seq_lengths = lengths[0]
    tok_dev = features.shape[1]
    width_here = features.shape[2]
    group_count = width_here // GW
    full_width = width_here * lax.axis_size("chan")
    ctx_pos = lax.axis_index("ctx")
    anchor = ctx_pos * tok_dev
    within = jnp.arange(tok_dev, dtype=jnp.int32)
    positions = anchor + within
    starts = segment_starts(seq_lengths, positions)

    rim_rows = from_behind(features[:, tok_dev - (SHORT - 1) :, :], "ctx", 1)
    extended = jnp.concatenate([rim_rows, features], axis=1)
    short_out = jnp.zeros((3, tok_dev, width_here), jnp.float32)
    for tap_index in range(SHORT):
        shifted = extended[:, SHORT - 1 - tap_index : SHORT - 1 - tap_index + tok_dev]
        usable = (positions - tap_index >= starts).astype(jnp.float32)
        short_out = (
            short_out
            + filters[:, tap_index, None, :] * shifted.astype(jnp.float32) * usable[None, :, None]
        )
    gated_prod = (short_out[1] * short_out[2]).astype(jnp.bfloat16)
    values = gated_prod.reshape(tok_dev, group_count, GW)

    last_start = starts[tok_dev - 1]
    kept_rows = (positions >= last_start).astype(jnp.float32)
    fading = (
        jnp.exp(-pole_rate[None] * (tok_dev - 1 - within)[:, None, None].astype(jnp.float32))
        * kept_rows[:, None, None]
    )
    fresh_state = jnp.einsum(
        "sgm,sgc->gmc", fading, values.astype(jnp.float32), precision=HIGHEST
    )
    through = jnp.where(last_start < anchor, jnp.exp(-pole_rate * tok_dev), 0.0)
    prior_state = prior_states(through, fresh_state, tok_dev)

    middle = tok_dev // 2
    offsets = (within - middle).astype(jnp.float32)
    left = residue_here[:, None, :] * jnp.exp(-pole_rate[:, None, :] * offsets[None, :, None])
    right = jnp.exp(pole_rate[:, :, None] * offsets[None, None, :])
    summed = jnp.einsum("gtm,gms->gts", left, right, precision=HIGHEST)
    inside = (within[None, :] <= within[:, None]) & (positions[None, :] >= starts[:, None])
    masked = jnp.where(inside[None], summed, 0.0).astype(jnp.bfloat16)
    intra_term = jnp.einsum("gts,sgc->tgc", masked, values, preferred_element_type=jnp.float32)

    carry_rows = (starts < anchor).astype(jnp.float32)
    reaching = (
        residue_here[None]
        * jnp.exp(-pole_rate[None] * (within + 1)[:, None, None].astype(jnp.float32))
        * carry_rows[:, None, None]
    )
    inter_term = jnp.einsum("tgm,gmc->tgc", reaching, prior_state, precision=HIGHEST)
    mixed_conv = (intra_term + inter_term).astype(jnp.bfloat16).reshape(tok_dev, width_here)

    activity = short_out[0] * mixed_conv.astype(jnp.float32)
    squares = butterfly_sum(jnp.sum(activity * activity, axis=1), "chan")
    normed = (
        activity * lax.rsqrt(squares[:, None] / full_width + EPSILON) * norm_gain[0][None, :]
    ).astype(jnp.bfloat16)
    handoff = from_behind_2(normed, "phase", 1)
    return handoff[None]


def solution(mesh):
    in_specs = (
        P("phase", None, "ctx", "chan"),
        P("phase", None, None, "chan"),
        P("phase", "chan", None),
        P("phase", "chan", None),
        P("phase", "chan"),
        P("phase", None),
    )
    out_specs = P("phase", "ctx", "chan")
    return jax.shard_map(
        on_device, mesh=mesh, in_specs=in_specs, out_specs=out_specs, check_vma=False
    )
```

```python
import jax
import jax.numpy as jnp
from jax import lax
from jax.sharding import PartitionSpec as P

GW = 128
SHORT = 3
LONGEST = 6144

EPSILON = 1e-05
HIGHEST = lax.Precision.HIGHEST


def from_behind(shard, axis, by):
    length = lax.axis_size(axis)
    pairs = [(i, i + by) for i in range(length) if 0 <= i + by < length]
    return lax.ppermute(shard, axis, pairs)


def from_behind_2(value, axis, steps):
    count = lax.axis_size(axis)
    pairs = [(source, (source + steps) % count) for source in range(count)]
    return lax.ppermute(value, axis, pairs)


def butterfly_sum(value, axis):
    count = lax.axis_size(axis)
    step = 1
    while step < count:
        pairs = [(i, i ^ step) for i in range(count)]
        value = value + lax.ppermute(value, axis, pairs)
        step *= 2
    return value


def segment_starts(seq_lengths, positions):
    starts = jnp.cumsum(seq_lengths) - seq_lengths
    chosen = jnp.where(starts[None, :] <= positions[:, None], starts[None, :], 0)
    return jnp.max(chosen, axis=1)


def prior_states(through, fresh, block_len):
    ctx_count = lax.axis_size("ctx")
    need = min(ctx_count, LONGEST // block_len + 1)
    groups, modes, lanes = fresh.shape
    decay_rows = (groups * modes) // lanes

    def pack(decay, state):
        return jnp.concatenate(
            [state.reshape(groups * modes, lanes), decay.reshape(decay_rows, lanes)], axis=0
        )

    def unpack(packed):
        state = packed[: groups * modes].reshape(groups, modes, lanes)
        decay = packed[groups * modes :].reshape(groups, modes)
        return decay, state

    inc_decay, inc_state = through, fresh
    exc_decay, exc_state = None, None
    cover = 1
    while True:
        got_decay, got_state = unpack(from_behind(pack(inc_decay, inc_state), "ctx", cover))
        if exc_state is None:
            exc_decay, exc_state = got_decay, got_state
        else:
            exc_state = exc_decay[..., None] * got_state + exc_state
            exc_decay = exc_decay * got_decay
        if 2 * cover - 1 >= need:
            return exc_state
        inc_state = inc_decay[..., None] * got_state + inc_state
        inc_decay = inc_decay * got_decay
        cover *= 2


def ring_sum(value, axis):
    count = lax.axis_size(axis)
    total = value
    for shift in range(1, count):
        pairs = [(i, (i + shift) % count) for i in range(count)]
        total = total + lax.ppermute(value, axis, pairs)
    return total


def on_device(projected, short_filter, decay_rate, residue, norm_gain, lengths):
    features = projected[0]
    filters = short_filter[0]
    pole_rate = decay_rate[0]
    residue_here = residue[0]
    seq_lengths = lengths[0]
    tok_dev = features.shape[1]
    width_here = features.shape[2]
    group_count = width_here // GW
    full_width = width_here * lax.axis_size("chan")
    ctx_pos = lax.axis_index("ctx")
    anchor = ctx_pos * tok_dev
    within = jnp.arange(tok_dev, dtype=jnp.int32)
    positions = anchor + within
    starts = segment_starts(seq_lengths, positions)

    rim_rows = from_behind(features[:, tok_dev - (SHORT - 1) :, :], "ctx", 1)
    extended = jnp.concatenate([rim_rows, features], axis=1)
    short_out = jnp.zeros((3, tok_dev, width_here), jnp.float32)
    for tap_index in range(SHORT):
        shifted = extended[:, SHORT - 1 - tap_index : SHORT - 1 - tap_index + tok_dev]
        usable = (positions - tap_index >= starts).astype(jnp.float32)
        short_out = (
            short_out
            + filters[:, tap_index, None, :] * shifted.astype(jnp.float32) * usable[None, :, None]
        )
    gated_prod = (short_out[1] * short_out[2]).astype(jnp.bfloat16)
    values = gated_prod.reshape(tok_dev, group_count, GW)

    last_start = starts[tok_dev - 1]
    kept_rows = (positions >= last_start).astype(jnp.float32)
    fading = (
        jnp.exp(-pole_rate[None] * (tok_dev - 1 - within)[:, None, None].astype(jnp.float32))
        * kept_rows[:, None, None]
    )
    fresh_state = jnp.einsum(
        "sgm,sgc->gmc", fading, values.astype(jnp.float32), precision=HIGHEST
    )
    through = jnp.where(last_start < anchor, jnp.exp(-pole_rate * tok_dev), 0.0)
    prior_state = prior_states(through, fresh_state, tok_dev)

    middle = tok_dev // 2
    offsets = (within - middle).astype(jnp.float32)
    left = residue_here[:, None, :] * jnp.exp(-pole_rate[:, None, :] * offsets[None, :, None])
    right = jnp.exp(pole_rate[:, :, None] * offsets[None, None, :])
    summed = jnp.einsum("gtm,gms->gts", left, right, precision=HIGHEST)
    inside = (within[None, :] <= within[:, None]) & (positions[None, :] >= starts[:, None])
    masked = jnp.where(inside[None], summed, 0.0).astype(jnp.bfloat16)
    intra_term = jnp.einsum("gts,sgc->tgc", masked, values, preferred_element_type=jnp.float32)

    carry_rows = (starts < anchor).astype(jnp.float32)
    reaching = (
        residue_here[None]
        * jnp.exp(-pole_rate[None] * (within + 1)[:, None, None].astype(jnp.float32))
        * carry_rows[:, None, None]
    )
    inter_term = jnp.einsum("tgm,gmc->tgc", reaching, prior_state, precision=HIGHEST)
    mixed_conv = (intra_term + inter_term).astype(jnp.bfloat16).reshape(tok_dev, width_here)

    activity = short_out[0] * mixed_conv.astype(jnp.float32)
    squares = ring_sum(jnp.sum(activity * activity, axis=1), "chan")
    normed = (
        activity * lax.rsqrt(squares[:, None] / full_width + EPSILON) * norm_gain[0][None, :]
    ).astype(jnp.bfloat16)
    handoff = from_behind_2(normed, "phase", 1)
    return handoff[None]


def solution(mesh):
    in_specs = (
        P("phase", None, "ctx", "chan"),
        P("phase", None, None, "chan"),
        P("phase", "chan", None),
        P("phase", "chan", None),
        P("phase", "chan"),
        P("phase", None),
    )
    out_specs = P("phase", "ctx", "chan")
    return jax.shard_map(
        on_device, mesh=mesh, in_specs=in_specs, out_specs=out_specs, check_vma=False
    )
```

```python
import jax
import jax.numpy as jnp
from jax import lax
from jax.sharding import PartitionSpec as P

GW = 128
SHORT = 3
LONGEST = 6144

EPSILON = 1e-05
HIGHEST = lax.Precision.HIGHEST


def from_behind(shard, axis, by):
    length = lax.axis_size(axis)
    pairs = [(i, i + by) for i in range(length) if 0 <= i + by < length]
    return lax.ppermute(shard, axis, pairs)


def from_behind_2(value, axis, steps):
    count = lax.axis_size(axis)
    pairs = [(source, (source + steps) % count) for source in range(count)]
    return lax.ppermute(value, axis, pairs)


def butterfly_sum(value, axis):
    count = lax.axis_size(axis)
    step = 1
    while step < count:
        pairs = [(i, i ^ step) for i in range(count)]
        value = value + lax.ppermute(value, axis, pairs)
        step *= 2
    return value


def segment_starts(seq_lengths, positions):
    result = jnp.zeros_like(positions)
    start = jnp.zeros((), seq_lengths.dtype)
    for index in range(seq_lengths.shape[0]):
        result = jnp.where(start <= positions, start, result)
        start = start + seq_lengths[index]
    return result


def prior_states(through, fresh, block_len):
    ctx_count = lax.axis_size("ctx")
    need = min(ctx_count, LONGEST // block_len + 1)
    groups, modes, lanes = fresh.shape
    decay_rows = (groups * modes) // lanes

    def pack(decay, state):
        return jnp.concatenate(
            [state.reshape(groups * modes, lanes), decay.reshape(decay_rows, lanes)], axis=0
        )

    def unpack(packed):
        state = packed[: groups * modes].reshape(groups, modes, lanes)
        decay = packed[groups * modes :].reshape(groups, modes)
        return decay, state

    inc_decay, inc_state = through, fresh
    exc_decay, exc_state = None, None
    cover = 1
    while True:
        got_decay, got_state = unpack(from_behind(pack(inc_decay, inc_state), "ctx", cover))
        if exc_state is None:
            if 2 * cover - 1 >= need:
                return jnp.ones_like(got_decay), jnp.zeros_like(got_state), got_state
            exc_decay, exc_state = got_decay, got_state
        else:
            if 2 * cover - 1 >= need:
                return exc_decay, exc_state, got_state
            exc_state = exc_decay[..., None] * got_state + exc_state
            exc_decay = exc_decay * got_decay
        inc_state = inc_decay[..., None] * got_state + inc_state
        inc_decay = inc_decay * got_decay
        cover *= 2


def ring_sum(value, axis):
    count = lax.axis_size(axis)
    total = value
    for shift in range(1, count):
        pairs = [(i, (i + shift) % count) for i in range(count)]
        total = total + lax.ppermute(value, axis, pairs)
    return total


def block_diagonal(state):
    groups, modes, lanes = state.shape
    same = jnp.arange(groups)[:, None] == jnp.arange(groups)[None, :]
    spread = jnp.where(same[:, None, :, None], state[:, :, None, :], 0.0)
    return spread.reshape(groups * modes, groups * lanes)


def on_device(projected, short_filter, decay_rate, residue, norm_gain, lengths):
    features = projected[0]
    filters = short_filter[0]
    pole_rate = decay_rate[0]
    residue_here = residue[0]
    seq_lengths = lengths[0]
    tok_dev = features.shape[1]
    width_here = features.shape[2]
    group_count = width_here // GW
    modes = pole_rate.shape[1]
    full_width = width_here * lax.axis_size("chan")
    ctx_pos = lax.axis_index("ctx")
    anchor = ctx_pos * tok_dev
    within = jnp.arange(tok_dev, dtype=jnp.int32)
    positions = anchor + within
    starts = segment_starts(seq_lengths, positions)

    rim_rows = from_behind(features[:, tok_dev - (SHORT - 1) :, :], "ctx", 1)
    extended = jnp.concatenate([rim_rows, features], axis=1)

    def short_conv(which):
        total = jnp.zeros((tok_dev, width_here), jnp.float32)
        for tap_index in range(SHORT):
            shifted = extended[which, SHORT - 1 - tap_index : SHORT - 1 - tap_index + tok_dev]
            usable = (positions - tap_index >= starts).astype(jnp.float32)
            total = total + filters[which, tap_index][None, :] * shifted.astype(
                jnp.float32
            ) * usable[:, None]
        return total

    gated_prod = (short_conv(1) * short_conv(2)).astype(jnp.bfloat16)
    values = gated_prod.reshape(tok_dev, group_count, GW)

    last_start = starts[tok_dev - 1]
    kept_rows = (positions >= last_start).astype(jnp.float32)
    fading = (
        jnp.exp(-pole_rate[None] * (tok_dev - 1 - within)[:, None, None].astype(jnp.float32))
        * kept_rows[:, None, None]
    )
    fresh_state = jnp.einsum(
        "sgm,sgc->gmc", fading, values.astype(jnp.float32), precision=HIGHEST
    )
    through = jnp.where(last_start < anchor, jnp.exp(-pole_rate * tok_dev), 0.0)
    earlier_decay, earlier_state, last_state = prior_states(through, fresh_state, tok_dev)

    middle = tok_dev // 2
    offsets = (within - middle).astype(jnp.float32)
    left = residue_here[:, None, :] * jnp.exp(-pole_rate[:, None, :] * offsets[None, :, None])
    right = jnp.exp(pole_rate[:, :, None] * offsets[None, None, :])
    summed = jnp.einsum("gtm,gms->gts", left, right, precision=HIGHEST)
    inside = (within[None, :] <= within[:, None]) & (positions[None, :] >= starts[:, None])
    masked = jnp.where(inside[None], summed, 0.0).astype(jnp.bfloat16)
    intra_term = jnp.einsum("gts,sgc->tgc", masked, values, preferred_element_type=jnp.float32)

    carry_rows = (starts < anchor).astype(jnp.float32)
    reaching = (
        residue_here[None]
        * jnp.exp(-pole_rate[None] * (within + 1)[:, None, None].astype(jnp.float32))
        * carry_rows[:, None, None]
    )
    flat_reach = reaching.reshape(tok_dev, group_count * modes)
    early_part = intra_term.reshape(tok_dev, width_here) + jnp.dot(
        flat_reach, block_diagonal(earlier_state), precision=HIGHEST
    )
    late_reach = (reaching * earlier_decay[None]).reshape(tok_dev, group_count * modes)
    inter_late = jnp.dot(late_reach, block_diagonal(last_state), precision=HIGHEST)
    mixed_conv = (early_part + inter_late).astype(jnp.bfloat16)

    activity = short_conv(0) * mixed_conv.astype(jnp.float32)
    squares = butterfly_sum(jnp.sum(activity * activity, axis=1), "chan")
    normed = (
        activity * lax.rsqrt(squares[:, None] / full_width + EPSILON) * norm_gain[0][None, :]
    ).astype(jnp.bfloat16)
    handoff = from_behind_2(normed, "phase", 1)
    return handoff[None]


def solution(mesh):
    in_specs = (
        P("phase", None, "ctx", "chan"),
        P("phase", None, None, "chan"),
        P("phase", "chan", None),
        P("phase", "chan", None),
        P("phase", "chan"),
        P("phase", None),
    )
    out_specs = P("phase", "ctx", "chan")
    return jax.shard_map(
        on_device, mesh=mesh, in_specs=in_specs, out_specs=out_specs, check_vma=False
    )
```

```python
import jax
import jax.numpy as jnp
from jax import lax
from jax.sharding import PartitionSpec as P

GW = 128
SHORT = 3
LONGEST = 6144

EPSILON = 1e-05
HIGHEST = lax.Precision.HIGHEST


def from_behind(shard, axis, by):
    length = lax.axis_size(axis)
    pairs = [(i, i + by) for i in range(length) if 0 <= i + by < length]
    return lax.ppermute(shard, axis, pairs)


def from_behind_2(value, axis, steps):
    count = lax.axis_size(axis)
    pairs = [(source, (source + steps) % count) for source in range(count)]
    return lax.ppermute(value, axis, pairs)


def butterfly_sum(value, axis):
    count = lax.axis_size(axis)
    step = 1
    while step < count:
        pairs = [(i, i ^ step) for i in range(count)]
        value = value + lax.ppermute(value, axis, pairs)
        step *= 2
    return value


def segment_starts(seq_lengths, positions):
    result = jnp.zeros_like(positions)
    start = jnp.zeros((), seq_lengths.dtype)
    for index in range(seq_lengths.shape[0]):
        result = jnp.where(start <= positions, start, result)
        start = start + seq_lengths[index]
    return result


def prior_states(fresh, pole_rate, keep, block_len):
    ctx_count = lax.axis_size("ctx")
    need = min(ctx_count, LONGEST // block_len + 1)
    groups, modes, lanes = fresh.shape
    ctx_pos = lax.axis_index("ctx")
    blocks = jnp.arange(ctx_count, dtype=jnp.int32)

    def decay_of(count):
        span = (blocks > ctx_pos - count) & (blocks <= ctx_pos)
        whole = jnp.all(jnp.where(span, keep, True)).astype(jnp.float32)
        return whole * jnp.exp(-pole_rate * float(count * block_len))

    def decay_before(count):
        span = (blocks >= ctx_pos - count) & (blocks < ctx_pos)
        whole = jnp.all(jnp.where(span, keep, True)).astype(jnp.float32)
        return whole * jnp.exp(-pole_rate * float(count * block_len))

    inc_state = fresh
    exc_state = jnp.zeros_like(fresh)
    cover = 1
    while True:
        got = from_behind(inc_state.reshape(groups * modes, lanes), "ctx", cover)
        got = got.reshape(groups, modes, lanes)
        exc_decay = decay_before(cover - 1)
        if 2 * cover - 1 >= need:
            return exc_decay, exc_state, got
        exc_state = exc_decay[..., None] * got + exc_state
        inc_state = decay_of(cover)[..., None] * got + inc_state
        cover *= 2


def ring_sum(value, axis):
    count = lax.axis_size(axis)
    total = value
    for shift in range(1, count):
        pairs = [(i, (i + shift) % count) for i in range(count)]
        total = total + lax.ppermute(value, axis, pairs)
    return total


def block_diagonal(state):
    groups, modes, lanes = state.shape
    same = jnp.arange(groups)[:, None] == jnp.arange(groups)[None, :]
    spread = jnp.where(same[:, None, :, None], state[:, :, None, :], 0.0)
    return spread.reshape(groups * modes, groups * lanes)


def on_device(projected, short_filter, decay_rate, residue, norm_gain, lengths):
    features = projected[0]
    filters = short_filter[0]
    pole_rate = decay_rate[0]
    residue_here = residue[0]
    seq_lengths = lengths[0]
    tok_dev = features.shape[1]
    width_here = features.shape[2]
    group_count = width_here // GW
    modes = pole_rate.shape[1]
    full_width = width_here * lax.axis_size("chan")
    ctx_pos = lax.axis_index("ctx")
    anchor = ctx_pos * tok_dev
    within = jnp.arange(tok_dev, dtype=jnp.int32)
    positions = anchor + within
    starts = segment_starts(seq_lengths, positions)

    rim_rows = from_behind(features[:, tok_dev - (SHORT - 1) :, :], "ctx", 1)
    extended = jnp.concatenate([rim_rows, features], axis=1)
    short_out = jnp.zeros((3, tok_dev, width_here), jnp.float32)
    for tap_index in range(SHORT):
        shifted = extended[:, SHORT - 1 - tap_index : SHORT - 1 - tap_index + tok_dev]
        usable = (positions - tap_index >= starts).astype(jnp.float32)
        short_out = (
            short_out
            + filters[:, tap_index, None, :] * shifted.astype(jnp.float32) * usable[None, :, None]
        )
    gated_prod = (short_out[1] * short_out[2]).astype(jnp.bfloat16)
    values = gated_prod.reshape(tok_dev, group_count, GW)

    last_start = starts[tok_dev - 1]
    kept_rows = (positions >= last_start).astype(jnp.float32)
    fading = (
        jnp.exp(-pole_rate[None] * (tok_dev - 1 - within)[:, None, None].astype(jnp.float32))
        * kept_rows[:, None, None]
    )
    fresh_state = jnp.einsum(
        "sgm,sgc->gmc", fading, values.astype(jnp.float32), precision=HIGHEST
    )
    ctx_count = lax.axis_size("ctx")
    block_first = jnp.arange(ctx_count, dtype=jnp.int32) * tok_dev
    keep = segment_starts(seq_lengths, block_first + tok_dev - 1) < block_first
    earlier_decay, earlier_state, last_state = prior_states(fresh_state, pole_rate, keep, tok_dev)

    middle = tok_dev // 2
    offsets = (within - middle).astype(jnp.float32)
    left = residue_here[:, None, :] * jnp.exp(-pole_rate[:, None, :] * offsets[None, :, None])
    right = jnp.exp(pole_rate[:, :, None] * offsets[None, None, :])
    summed = jnp.einsum("gtm,gms->gts", left, right, precision=HIGHEST)
    inside = (within[None, :] <= within[:, None]) & (positions[None, :] >= starts[:, None])
    masked = jnp.where(inside[None], summed, 0.0).astype(jnp.bfloat16)
    intra_term = jnp.einsum("gts,sgc->tgc", masked, values, preferred_element_type=jnp.float32)

    carry_rows = (starts < anchor).astype(jnp.float32)
    reaching = (
        residue_here[None]
        * jnp.exp(-pole_rate[None] * (within + 1)[:, None, None].astype(jnp.float32))
        * carry_rows[:, None, None]
    )
    flat_reach = reaching.reshape(tok_dev, group_count * modes)
    early_part = intra_term.reshape(tok_dev, width_here) + jnp.dot(
        flat_reach, block_diagonal(earlier_state), precision=HIGHEST
    )
    late_reach = (reaching * earlier_decay[None]).reshape(tok_dev, group_count * modes)
    inter_late = jnp.dot(late_reach, block_diagonal(last_state), precision=HIGHEST)
    mixed_conv = (early_part + inter_late).astype(jnp.bfloat16)

    activity = short_out[0] * mixed_conv.astype(jnp.float32)
    squares = butterfly_sum(jnp.sum(activity * activity, axis=1), "chan")
    normed = (
        activity * lax.rsqrt(squares[:, None] / full_width + EPSILON) * norm_gain[0][None, :]
    ).astype(jnp.bfloat16)
    handoff = from_behind_2(normed, "phase", 1)
    return handoff[None]


def solution(mesh):
    in_specs = (
        P("phase", None, "ctx", "chan"),
        P("phase", None, None, "chan"),
        P("phase", "chan", None),
        P("phase", "chan", None),
        P("phase", "chan"),
        P("phase", None),
    )
    out_specs = P("phase", "ctx", "chan")
    return jax.shard_map(
        on_device, mesh=mesh, in_specs=in_specs, out_specs=out_specs, check_vma=False
    )
```

```python
import jax
import jax.numpy as jnp
from jax import lax
from jax.sharding import PartitionSpec as P

GW = 128
SHORT = 3
LONGEST = 6144

EPSILON = 1e-05
HIGHEST = lax.Precision.HIGHEST
HIGH = lax.Precision.HIGH


def from_behind(shard, axis, by):
    length = lax.axis_size(axis)
    pairs = [(i, i + by) for i in range(length) if 0 <= i + by < length]
    return lax.ppermute(shard, axis, pairs)


def from_behind_2(value, axis, steps):
    count = lax.axis_size(axis)
    pairs = [(source, (source + steps) % count) for source in range(count)]
    return lax.ppermute(value, axis, pairs)


def butterfly_sum(value, axis):
    count = lax.axis_size(axis)
    step = 1
    while step < count:
        pairs = [(i, i ^ step) for i in range(count)]
        value = value + lax.ppermute(value, axis, pairs)
        step *= 2
    return value


def segment_starts(seq_lengths, positions):
    result = jnp.zeros_like(positions)
    start = jnp.zeros((), seq_lengths.dtype)
    for index in range(seq_lengths.shape[0]):
        result = jnp.where(start <= positions, start, result)
        start = start + seq_lengths[index]
    return result


def prior_states(fresh, pole_rate, keep, block_len):
    ctx_count = lax.axis_size("ctx")
    need = min(ctx_count, LONGEST // block_len + 1)
    groups, modes, lanes = fresh.shape
    ctx_pos = lax.axis_index("ctx")
    blocks = jnp.arange(ctx_count, dtype=jnp.int32)

    def decay_of(count):
        span = (blocks > ctx_pos - count) & (blocks <= ctx_pos)
        whole = jnp.all(jnp.where(span, keep, True)).astype(jnp.float32)
        return whole * jnp.exp(-pole_rate * float(count * block_len))

    def decay_before(count):
        span = (blocks >= ctx_pos - count) & (blocks < ctx_pos)
        whole = jnp.all(jnp.where(span, keep, True)).astype(jnp.float32)
        return whole * jnp.exp(-pole_rate * float(count * block_len))

    inc_state = fresh
    exc_state = jnp.zeros_like(fresh)
    cover = 1
    while True:
        sent = inc_state.reshape(groups * modes, lanes).astype(jnp.bfloat16)
        got = from_behind(sent, "ctx", cover).astype(jnp.float32)
        got = got.reshape(groups, modes, lanes)
        exc_decay = decay_before(cover - 1)
        if 2 * cover - 1 >= need:
            return exc_decay, exc_state, got
        exc_state = exc_decay[..., None] * got + exc_state
        inc_state = decay_of(cover)[..., None] * got + inc_state
        cover *= 2


def ring_sum(value, axis):
    count = lax.axis_size(axis)
    total = value
    for shift in range(1, count):
        pairs = [(i, (i + shift) % count) for i in range(count)]
        total = total + lax.ppermute(value, axis, pairs)
    return total


def block_diagonal(state):
    groups, modes, lanes = state.shape
    same = jnp.arange(groups)[:, None] == jnp.arange(groups)[None, :]
    spread = jnp.where(same[:, None, :, None], state[:, :, None, :], 0.0)
    return spread.reshape(groups * modes, groups * lanes)


def on_device(projected, short_filter, decay_rate, residue, norm_gain, lengths):
    features = projected[0]
    filters = short_filter[0]
    pole_rate = decay_rate[0]
    residue_here = residue[0]
    seq_lengths = lengths[0]
    tok_dev = features.shape[1]
    width_here = features.shape[2]
    group_count = width_here // GW
    modes = pole_rate.shape[1]
    full_width = width_here * lax.axis_size("chan")
    ctx_pos = lax.axis_index("ctx")
    anchor = ctx_pos * tok_dev
    within = jnp.arange(tok_dev, dtype=jnp.int32)
    positions = anchor + within
    starts = segment_starts(seq_lengths, positions)

    rim_rows = from_behind(features[:, tok_dev - (SHORT - 1) :, :], "ctx", 1)
    extended = jnp.concatenate([rim_rows, features], axis=1)
    short_out = jnp.zeros((3, tok_dev, width_here), jnp.float32)
    for tap_index in range(SHORT):
        shifted = extended[:, SHORT - 1 - tap_index : SHORT - 1 - tap_index + tok_dev]
        usable = (positions - tap_index >= starts).astype(jnp.float32)
        short_out = (
            short_out
            + filters[:, tap_index, None, :] * shifted.astype(jnp.float32) * usable[None, :, None]
        )
    gated_prod = (short_out[1] * short_out[2]).astype(jnp.bfloat16)
    values = gated_prod.reshape(tok_dev, group_count, GW)

    last_start = starts[tok_dev - 1]
    kept_rows = (positions >= last_start).astype(jnp.float32)
    fading = (
        jnp.exp(-pole_rate[None] * (tok_dev - 1 - within)[:, None, None].astype(jnp.float32))
        * kept_rows[:, None, None]
    )
    fresh_state = jnp.einsum(
        "sgm,sgc->gmc", fading, values.astype(jnp.float32), precision=HIGHEST
    )
    ctx_count = lax.axis_size("ctx")
    block_first = jnp.arange(ctx_count, dtype=jnp.int32) * tok_dev
    keep = segment_starts(seq_lengths, block_first + tok_dev - 1) < block_first
    earlier_decay, earlier_state, last_state = prior_states(fresh_state, pole_rate, keep, tok_dev)

    middle = tok_dev // 2
    offsets = (within - middle).astype(jnp.float32)
    left = residue_here[:, None, :] * jnp.exp(-pole_rate[:, None, :] * offsets[None, :, None])
    right = jnp.exp(pole_rate[:, :, None] * offsets[None, None, :])
    summed = jnp.einsum("gtm,gms->gts", left, right, precision=HIGHEST)
    inside = (within[None, :] <= within[:, None]) & (positions[None, :] >= starts[:, None])
    masked = jnp.where(inside[None], summed, 0.0).astype(jnp.bfloat16)
    intra_term = jnp.einsum("gts,sgc->tgc", masked, values, preferred_element_type=jnp.float32)

    carry_rows = (starts < anchor).astype(jnp.float32)
    reaching = (
        residue_here[None]
        * jnp.exp(-pole_rate[None] * (within + 1)[:, None, None].astype(jnp.float32))
        * carry_rows[:, None, None]
    )
    flat_reach = reaching.reshape(tok_dev, group_count * modes)
    early_part = intra_term.reshape(tok_dev, width_here) + jnp.dot(
        flat_reach, block_diagonal(earlier_state), precision=HIGH
    )
    late_reach = (reaching * earlier_decay[None]).reshape(tok_dev, group_count * modes)
    inter_late = jnp.dot(late_reach, block_diagonal(last_state), precision=HIGH)
    mixed_conv = (early_part + inter_late).astype(jnp.bfloat16)

    activity = short_out[0] * mixed_conv.astype(jnp.float32)
    squares = butterfly_sum(jnp.sum(activity * activity, axis=1), "chan")
    normed = (
        activity * lax.rsqrt(squares[:, None] / full_width + EPSILON) * norm_gain[0][None, :]
    ).astype(jnp.bfloat16)
    handoff = from_behind_2(normed, "phase", 1)
    return handoff[None]


def solution(mesh):
    in_specs = (
        P("phase", None, "ctx", "chan"),
        P("phase", None, None, "chan"),
        P("phase", "chan", None),
        P("phase", "chan", None),
        P("phase", "chan"),
        P("phase", None),
    )
    out_specs = P("phase", "ctx", "chan")
    return jax.shard_map(
        on_device, mesh=mesh, in_specs=in_specs, out_specs=out_specs, check_vma=False
    )
```

```python
import jax
import jax.numpy as jnp
from jax import lax
from jax.sharding import PartitionSpec as P

GW = 128
SHORT = 3
LONGEST = 6144

EPSILON = 1e-05
HIGHEST = lax.Precision.HIGHEST
HIGH = lax.Precision.HIGH


def from_behind(shard, axis, by):
    length = lax.axis_size(axis)
    pairs = [(i, i + by) for i in range(length) if 0 <= i + by < length]
    return lax.ppermute(shard, axis, pairs)


def from_behind_2(value, axis, steps):
    count = lax.axis_size(axis)
    pairs = [(source, (source + steps) % count) for source in range(count)]
    return lax.ppermute(value, axis, pairs)


def butterfly_sum(value, axis):
    count = lax.axis_size(axis)
    step = 1
    while step < count:
        pairs = [(i, i ^ step) for i in range(count)]
        value = value + lax.ppermute(value, axis, pairs)
        step *= 2
    return value


def segment_starts(seq_lengths, positions):
    result = jnp.zeros_like(positions)
    start = jnp.zeros((), seq_lengths.dtype)
    for index in range(seq_lengths.shape[0]):
        result = jnp.where(start <= positions, start, result)
        start = start + seq_lengths[index]
    return result


def prior_state(fresh, pole_rate, keep, block_len):
    ctx_count = lax.axis_size("ctx")
    window = min(ctx_count, LONGEST // block_len + 1)
    ctx_pos = lax.axis_index("ctx")
    blocks = jnp.arange(ctx_count, dtype=jnp.int32)
    gathered = lax.all_gather(fresh.astype(jnp.bfloat16), "ctx")
    padded = jnp.concatenate([jnp.zeros((window,) + fresh.shape, jnp.bfloat16), gathered], axis=0)
    recent = lax.dynamic_slice_in_dim(padded, ctx_pos, window, 0).astype(jnp.float32)
    back = jnp.arange(window, dtype=jnp.int32)
    first = ctx_pos - window + back
    span = (blocks[None, :] > first[:, None]) & (blocks[None, :] < ctx_pos)
    whole = jnp.all(jnp.where(span, keep[None, :], True), axis=1).astype(jnp.float32)
    lag = (window - 1 - back).astype(jnp.float32) * block_len
    weight = whole[:, None, None] * jnp.exp(-pole_rate[None] * lag[:, None, None])
    return jnp.sum(weight[..., None] * recent, axis=0)


def ring_sum(value, axis):
    count = lax.axis_size(axis)
    total = value
    for shift in range(1, count):
        pairs = [(i, (i + shift) % count) for i in range(count)]
        total = total + lax.ppermute(value, axis, pairs)
    return total


def block_diagonal(state):
    groups, modes, lanes = state.shape
    same = jnp.arange(groups)[:, None] == jnp.arange(groups)[None, :]
    spread = jnp.where(same[:, None, :, None], state[:, :, None, :], 0.0)
    return spread.reshape(groups * modes, groups * lanes)


def on_device(projected, short_filter, decay_rate, residue, norm_gain, lengths):
    features = projected[0]
    filters = short_filter[0]
    pole_rate = decay_rate[0]
    residue_here = residue[0]
    seq_lengths = lengths[0]
    tok_dev = features.shape[1]
    width_here = features.shape[2]
    group_count = width_here // GW
    modes = pole_rate.shape[1]
    full_width = width_here * lax.axis_size("chan")
    ctx_pos = lax.axis_index("ctx")
    anchor = ctx_pos * tok_dev
    within = jnp.arange(tok_dev, dtype=jnp.int32)
    positions = anchor + within
    starts = segment_starts(seq_lengths, positions)

    rim_rows = from_behind(features[:, tok_dev - (SHORT - 1) :, :], "ctx", 1)
    extended = jnp.concatenate([rim_rows, features], axis=1)
    short_out = jnp.zeros((3, tok_dev, width_here), jnp.float32)
    for tap_index in range(SHORT):
        shifted = extended[:, SHORT - 1 - tap_index : SHORT - 1 - tap_index + tok_dev]
        usable = (positions - tap_index >= starts).astype(jnp.float32)
        short_out = (
            short_out
            + filters[:, tap_index, None, :] * shifted.astype(jnp.float32) * usable[None, :, None]
        )
    gated_prod = (short_out[1] * short_out[2]).astype(jnp.bfloat16)
    values = gated_prod.reshape(tok_dev, group_count, GW)

    last_start = starts[tok_dev - 1]
    kept_rows = (positions >= last_start).astype(jnp.float32)
    fading = (
        jnp.exp(-pole_rate[None] * (tok_dev - 1 - within)[:, None, None].astype(jnp.float32))
        * kept_rows[:, None, None]
    )
    fresh_state = jnp.einsum(
        "sgm,sgc->gmc", fading, values.astype(jnp.float32), precision=HIGHEST
    )
    ctx_count = lax.axis_size("ctx")
    block_first = jnp.arange(ctx_count, dtype=jnp.int32) * tok_dev
    keep = segment_starts(seq_lengths, block_first + tok_dev - 1) < block_first
    state_before = prior_state(fresh_state, pole_rate, keep, tok_dev)

    middle = tok_dev // 2
    offsets = (within - middle).astype(jnp.float32)
    left = residue_here[:, None, :] * jnp.exp(-pole_rate[:, None, :] * offsets[None, :, None])
    right = jnp.exp(pole_rate[:, :, None] * offsets[None, None, :])
    summed = jnp.einsum("gtm,gms->gts", left, right, precision=HIGHEST)
    inside = (within[None, :] <= within[:, None]) & (positions[None, :] >= starts[:, None])
    masked = jnp.where(inside[None], summed, 0.0).astype(jnp.bfloat16)
    intra_term = jnp.einsum("gts,sgc->tgc", masked, values, preferred_element_type=jnp.float32)

    carry_rows = (starts < anchor).astype(jnp.float32)
    reaching = (
        residue_here[None]
        * jnp.exp(-pole_rate[None] * (within + 1)[:, None, None].astype(jnp.float32))
        * carry_rows[:, None, None]
    )
    flat_reach = reaching.reshape(tok_dev, group_count * modes)
    inter_term = jnp.dot(flat_reach, block_diagonal(state_before), precision=HIGH)
    mixed_conv = (intra_term.reshape(tok_dev, width_here) + inter_term).astype(jnp.bfloat16)

    activity = short_out[0] * mixed_conv.astype(jnp.float32)
    squares = butterfly_sum(jnp.sum(activity * activity, axis=1), "chan")
    normed = (
        activity * lax.rsqrt(squares[:, None] / full_width + EPSILON) * norm_gain[0][None, :]
    ).astype(jnp.bfloat16)
    handoff = from_behind_2(normed, "phase", 1)
    return handoff[None]


def solution(mesh):
    in_specs = (
        P("phase", None, "ctx", "chan"),
        P("phase", None, None, "chan"),
        P("phase", "chan", None),
        P("phase", "chan", None),
        P("phase", "chan"),
        P("phase", None),
    )
    out_specs = P("phase", "ctx", "chan")
    return jax.shard_map(
        on_device, mesh=mesh, in_specs=in_specs, out_specs=out_specs, check_vma=False
    )
```

```python
import jax
import jax.numpy as jnp
from jax import lax
from jax.sharding import PartitionSpec as P

GW = 128
SHORT = 3
LONGEST = 6144

EPSILON = 1e-05
HIGHEST = lax.Precision.HIGHEST
HIGH = lax.Precision.HIGH


def from_behind(shard, axis, by):
    length = lax.axis_size(axis)
    pairs = [(i, i + by) for i in range(length) if 0 <= i + by < length]
    return lax.ppermute(shard, axis, pairs)


def from_behind_2(value, axis, steps):
    count = lax.axis_size(axis)
    pairs = [(source, (source + steps) % count) for source in range(count)]
    return lax.ppermute(value, axis, pairs)


def butterfly_sum(value, axis):
    count = lax.axis_size(axis)
    step = 1
    while step < count:
        pairs = [(i, i ^ step) for i in range(count)]
        value = value + lax.ppermute(value, axis, pairs)
        step *= 2
    return value


def segment_starts(seq_lengths, positions):
    count = seq_lengths.shape[0]
    before = jnp.arange(count)[:, None] < jnp.arange(count)[None, :]
    starts = jnp.sum(jnp.where(before, seq_lengths[:, None], 0), axis=0)
    chosen = jnp.where(starts[None, :] <= positions[:, None], starts[None, :], 0)
    return jnp.max(chosen, axis=1)


def prior_states(fresh, pole_rate, keep, block_len):
    ctx_count = lax.axis_size("ctx")
    need = min(ctx_count, LONGEST // block_len + 1)
    groups, modes, lanes = fresh.shape
    ctx_pos = lax.axis_index("ctx")
    blocks = jnp.arange(ctx_count, dtype=jnp.int32)

    covers = []
    cover = 1
    while True:
        covers.append(cover)
        if 2 * cover - 1 >= need:
            break
        cover *= 2
    spans = []
    for cover in covers:
        spans.append((1 - cover, -1, cover - 1))
        spans.append((1 - cover, 0, cover))
    first = jnp.array([sp[0] for sp in spans], jnp.int32) + ctx_pos
    last = jnp.array([sp[1] for sp in spans], jnp.int32) + ctx_pos
    length = jnp.array([float(sp[2] * block_len) for sp in spans], jnp.float32)
    inside = (blocks[None, :] >= first[:, None]) & (blocks[None, :] <= last[:, None])
    whole = jnp.min(jnp.where(inside, keep.astype(jnp.float32)[None, :], 1.0), axis=1)
    decays = whole[:, None, None] * jnp.exp(-pole_rate[None] * length[:, None, None])

    inc_state = fresh
    exc_state = jnp.zeros_like(fresh)
    for index, cover in enumerate(covers):
        sent = inc_state.reshape(groups * modes, lanes).astype(jnp.bfloat16)
        got = from_behind(sent, "ctx", cover).astype(jnp.float32)
        got = got.reshape(groups, modes, lanes)
        exc_decay = decays[2 * index]
        if index == len(covers) - 1:
            return exc_decay, exc_state, got
        exc_state = exc_decay[..., None] * got + exc_state
        inc_state = decays[2 * index + 1][..., None] * got + inc_state


def ring_sum(value, axis):
    count = lax.axis_size(axis)
    total = value
    for shift in range(1, count):
        pairs = [(i, (i + shift) % count) for i in range(count)]
        total = total + lax.ppermute(value, axis, pairs)
    return total


def block_diagonal(state):
    groups, modes, lanes = state.shape
    same = jnp.arange(groups)[:, None] == jnp.arange(groups)[None, :]
    spread = jnp.where(same[:, None, :, None], state[:, :, None, :], 0.0)
    return spread.reshape(groups * modes, groups * lanes)


def on_device(projected, short_filter, decay_rate, residue, norm_gain, lengths):
    features = projected[0]
    filters = short_filter[0]
    pole_rate = decay_rate[0]
    residue_here = residue[0]
    seq_lengths = lengths[0]
    tok_dev = features.shape[1]
    width_here = features.shape[2]
    group_count = width_here // GW
    modes = pole_rate.shape[1]
    full_width = width_here * lax.axis_size("chan")
    ctx_pos = lax.axis_index("ctx")
    anchor = ctx_pos * tok_dev
    within = jnp.arange(tok_dev, dtype=jnp.int32)
    positions = anchor + within
    starts = segment_starts(seq_lengths, positions)

    rim_rows = from_behind(features[:, tok_dev - (SHORT - 1) :, :], "ctx", 1)
    extended = jnp.concatenate([rim_rows, features], axis=1)
    short_out = jnp.zeros((3, tok_dev, width_here), jnp.float32)
    for tap_index in range(SHORT):
        shifted = extended[:, SHORT - 1 - tap_index : SHORT - 1 - tap_index + tok_dev]
        usable = (positions - tap_index >= starts).astype(jnp.float32)
        short_out = (
            short_out
            + filters[:, tap_index, None, :] * shifted.astype(jnp.float32) * usable[None, :, None]
        )
    gated_prod = (short_out[1] * short_out[2]).astype(jnp.bfloat16)
    values = gated_prod.reshape(tok_dev, group_count, GW)

    last_start = starts[tok_dev - 1]
    kept_rows = (positions >= last_start).astype(jnp.float32)
    fading = (
        jnp.exp(-pole_rate[None] * (tok_dev - 1 - within)[:, None, None].astype(jnp.float32))
        * kept_rows[:, None, None]
    )
    fresh_state = jnp.einsum(
        "sgm,sgc->gmc", fading, values.astype(jnp.float32), precision=HIGHEST
    )
    ctx_count = lax.axis_size("ctx")
    block_first = jnp.arange(ctx_count, dtype=jnp.int32) * tok_dev
    keep = segment_starts(seq_lengths, block_first + tok_dev - 1) < block_first
    earlier_decay, earlier_state, last_state = prior_states(fresh_state, pole_rate, keep, tok_dev)

    middle = tok_dev // 2
    offsets = (within - middle).astype(jnp.float32)
    left = residue_here[:, None, :] * jnp.exp(-pole_rate[:, None, :] * offsets[None, :, None])
    right = jnp.exp(pole_rate[:, :, None] * offsets[None, None, :])
    summed = jnp.einsum("gtm,gms->gts", left, right, precision=HIGHEST)
    inside = (within[None, :] <= within[:, None]) & (positions[None, :] >= starts[:, None])
    masked = jnp.where(inside[None], summed, 0.0).astype(jnp.bfloat16)
    intra_term = jnp.einsum("gts,sgc->tgc", masked, values, preferred_element_type=jnp.float32)

    carry_rows = (starts < anchor).astype(jnp.float32)
    reaching = (
        residue_here[None]
        * jnp.exp(-pole_rate[None] * (within + 1)[:, None, None].astype(jnp.float32))
        * carry_rows[:, None, None]
    )
    flat_reach = reaching.reshape(tok_dev, group_count * modes)
    early_part = intra_term.reshape(tok_dev, width_here) + jnp.dot(
        flat_reach, block_diagonal(earlier_state), precision=HIGH
    )
    late_reach = (reaching * earlier_decay[None]).reshape(tok_dev, group_count * modes)
    inter_late = jnp.dot(late_reach, block_diagonal(last_state), precision=HIGH)
    mixed_conv = (early_part + inter_late).astype(jnp.bfloat16)

    activity = short_out[0] * mixed_conv.astype(jnp.float32)
    squares = butterfly_sum(jnp.sum(activity * activity, axis=1), "chan")
    normed = (
        activity * lax.rsqrt(squares[:, None] / full_width + EPSILON) * norm_gain[0][None, :]
    ).astype(jnp.bfloat16)
    handoff = from_behind_2(normed, "phase", 1)
    return handoff[None]


def solution(mesh):
    in_specs = (
        P("phase", None, "ctx", "chan"),
        P("phase", None, None, "chan"),
        P("phase", "chan", None),
        P("phase", "chan", None),
        P("phase", "chan"),
        P("phase", None),
    )
    out_specs = P("phase", "ctx", "chan")
    return jax.shard_map(
        on_device, mesh=mesh, in_specs=in_specs, out_specs=out_specs, check_vma=False
    )
```

```python
import jax
import jax.numpy as jnp
from jax import lax
from jax.sharding import PartitionSpec as P

GW = 128
SHORT = 3
LONGEST = 6144

EPSILON = 1e-05
HIGHEST = lax.Precision.HIGHEST
HIGH = lax.Precision.HIGH


def from_behind(shard, axis, by):
    length = lax.axis_size(axis)
    pairs = [(i, i + by) for i in range(length) if 0 <= i + by < length]
    return lax.ppermute(shard, axis, pairs)


def from_behind_2(value, axis, steps):
    count = lax.axis_size(axis)
    pairs = [(source, (source + steps) % count) for source in range(count)]
    return lax.ppermute(value, axis, pairs)


def butterfly_sum(value, axis):
    count = lax.axis_size(axis)
    step = 1
    while step < count:
        pairs = [(i, i ^ step) for i in range(count)]
        value = value + lax.ppermute(value, axis, pairs)
        step *= 2
    return value


def segment_starts(seq_lengths, positions):
    count = seq_lengths.shape[0]
    before = jnp.arange(count)[:, None] < jnp.arange(count)[None, :]
    starts = jnp.sum(jnp.where(before, seq_lengths[:, None], 0), axis=0)
    chosen = jnp.where(starts[None, :] <= positions[:, None], starts[None, :], 0)
    return jnp.max(chosen, axis=1)


def prior_states(fresh, pole_rate, keep, block_len):
    ctx_count = lax.axis_size("ctx")
    need = min(ctx_count, LONGEST // block_len + 1)
    groups, modes, lanes = fresh.shape
    ctx_pos = lax.axis_index("ctx")
    blocks = jnp.arange(ctx_count, dtype=jnp.int32)

    covers = []
    cover = 1
    while True:
        covers.append(cover)
        if 2 * cover - 1 >= need:
            break
        cover *= 2
    spans = []
    for cover in covers:
        spans.append((1 - cover, -1, cover - 1))
        spans.append((1 - cover, 0, cover))
    first = jnp.array([sp[0] for sp in spans], jnp.int32) + ctx_pos
    last = jnp.array([sp[1] for sp in spans], jnp.int32) + ctx_pos
    length = jnp.array([float(sp[2] * block_len) for sp in spans], jnp.float32)
    inside = (blocks[None, :] >= first[:, None]) & (blocks[None, :] <= last[:, None])
    whole = jnp.min(jnp.where(inside, keep.astype(jnp.float32)[None, :], 1.0), axis=1)
    decays = whole[:, None, None] * jnp.exp(-pole_rate[None] * length[:, None, None])

    inc_state = fresh
    exc_state = jnp.zeros_like(fresh)
    for index, cover in enumerate(covers):
        sent = inc_state.reshape(groups * modes, lanes).astype(jnp.bfloat16)
        got = from_behind(sent, "ctx", cover).astype(jnp.float32)
        got = got.reshape(groups, modes, lanes)
        exc_decay = decays[2 * index]
        if index == len(covers) - 1:
            return exc_decay, exc_state, got
        exc_state = exc_decay[..., None] * got + exc_state
        inc_state = decays[2 * index + 1][..., None] * got + inc_state


def ring_sum(value, axis):
    count = lax.axis_size(axis)
    total = value
    for shift in range(1, count):
        pairs = [(i, (i + shift) % count) for i in range(count)]
        total = total + lax.ppermute(value, axis, pairs)
    return total


def block_diagonal(state):
    groups, modes, lanes = state.shape
    same = jnp.arange(groups)[:, None] == jnp.arange(groups)[None, :]
    spread = jnp.where(same[:, None, :, None], state[:, :, None, :], 0.0)
    return spread.reshape(groups * modes, groups * lanes)


def on_device(projected, short_filter, decay_rate, residue, norm_gain, lengths):
    features = projected[0]
    filters = short_filter[0]
    pole_rate = decay_rate[0]
    residue_here = residue[0]
    seq_lengths = lengths[0]
    tok_dev = features.shape[1]
    width_here = features.shape[2]
    group_count = width_here // GW
    modes = pole_rate.shape[1]
    full_width = width_here * lax.axis_size("chan")
    ctx_pos = lax.axis_index("ctx")
    anchor = ctx_pos * tok_dev
    within = jnp.arange(tok_dev, dtype=jnp.int32)
    positions = anchor + within
    starts = segment_starts(seq_lengths, positions)

    rim_rows = from_behind(features[:, tok_dev - (SHORT - 1) :, :], "ctx", 1)
    extended = jnp.concatenate([rim_rows, features], axis=1)
    short_out = jnp.zeros((3, tok_dev, width_here), jnp.float32)
    for tap_index in range(SHORT):
        shifted = extended[:, SHORT - 1 - tap_index : SHORT - 1 - tap_index + tok_dev]
        usable = (positions - tap_index >= starts).astype(jnp.float32)
        short_out = (
            short_out
            + filters[:, tap_index, None, :] * shifted.astype(jnp.float32) * usable[None, :, None]
        )
    gated_prod = (short_out[1] * short_out[2]).astype(jnp.bfloat16)
    values = gated_prod.reshape(tok_dev, group_count, GW)

    last_start = starts[tok_dev - 1]
    kept_rows = (positions >= last_start).astype(jnp.float32)
    fading = (
        jnp.exp(-pole_rate[None] * (tok_dev - 1 - within)[:, None, None].astype(jnp.float32))
        * kept_rows[:, None, None]
    )
    fresh_state = jnp.einsum(
        "sgm,sgc->gmc", fading, values.astype(jnp.float32), precision=HIGHEST
    )
    ctx_count = lax.axis_size("ctx")
    block_first = jnp.arange(ctx_count, dtype=jnp.int32) * tok_dev
    keep = segment_starts(seq_lengths, block_first + tok_dev - 1) < block_first
    earlier_decay, earlier_state, last_state = prior_states(fresh_state, pole_rate, keep, tok_dev)

    middle = tok_dev // 2
    offsets = (within - middle).astype(jnp.float32)
    left = residue_here[:, None, :] * jnp.exp(-pole_rate[:, None, :] * offsets[None, :, None])
    right = jnp.exp(pole_rate[:, :, None] * offsets[None, None, :])
    summed = jnp.einsum("gtm,gms->gts", left, right, precision=HIGHEST)
    inside = (within[None, :] <= within[:, None]) & (positions[None, :] >= starts[:, None])
    masked = jnp.where(inside[None], summed, 0.0).astype(jnp.bfloat16)
    intra_term = jnp.einsum("gts,sgc->tgc", masked, values, preferred_element_type=jnp.float32)

    carry_rows = (starts < anchor).astype(jnp.float32)
    reaching = (
        residue_here[None]
        * jnp.exp(-pole_rate[None] * (within + 1)[:, None, None].astype(jnp.float32))
        * carry_rows[:, None, None]
    )
    flat_reach = reaching.reshape(tok_dev, group_count * modes)
    early_part = intra_term.reshape(tok_dev, width_here) + jnp.dot(
        flat_reach, block_diagonal(earlier_state), precision=HIGH
    )
    late_reach = (reaching * earlier_decay[None]).reshape(tok_dev, group_count * modes)
    inter_late = jnp.dot(late_reach, block_diagonal(last_state), precision=HIGH)
    mixed_conv = (early_part + inter_late).astype(jnp.bfloat16)

    activity = short_out[0] * mixed_conv.astype(jnp.float32)
    squares = lax.psum(jnp.sum(activity * activity, axis=1), "chan")
    normed = (
        activity * lax.rsqrt(squares[:, None] / full_width + EPSILON) * norm_gain[0][None, :]
    ).astype(jnp.bfloat16)
    handoff = from_behind_2(normed, "phase", 1)
    return handoff[None]


def solution(mesh):
    in_specs = (
        P("phase", None, "ctx", "chan"),
        P("phase", None, None, "chan"),
        P("phase", "chan", None),
        P("phase", "chan", None),
        P("phase", "chan"),
        P("phase", None),
    )
    out_specs = P("phase", "ctx", "chan")
    return jax.shard_map(
        on_device, mesh=mesh, in_specs=in_specs, out_specs=out_specs, check_vma=False
    )
```

```python
import jax
import jax.numpy as jnp
from jax import lax
from jax.sharding import PartitionSpec as P
from jax.experimental import pallas as pl
from jax.experimental.pallas import tpu as pltpu

GW = 128
SHORT = 3
LONGEST = 6144

EPSILON = 1e-05
HIGHEST = lax.Precision.HIGHEST
HIGH = lax.Precision.HIGH


CONV_TILE = 512


def conv_kernel(feat_ref, rim_ref, filt_ref, use_ref, gated_ref, query_ref):
    tok_dev, tile = gated_ref.shape
    rows = lax.broadcasted_iota(jnp.int32, (tok_dev, tile), 0)
    outs = []
    for which in range(3):
        plain = feat_ref[which].astype(jnp.float32)
        rim = rim_ref[which].astype(jnp.float32)
        total = jnp.zeros((tok_dev, tile), jnp.float32)
        for tap_index in range(SHORT):
            shifted = plain
            if tap_index:
                shifted = pltpu.roll(plain, tap_index, 0)
                for row in range(tap_index):
                    shifted = jnp.where(
                        rows == row, rim[SHORT - 1 - tap_index + row][None, :], shifted
                    )
            total = total + filt_ref[which, tap_index][None, :] * shifted * use_ref[tap_index]
        outs.append(total)
    gated_ref[...] = (outs[1] * outs[2]).astype(jnp.bfloat16)
    query_ref[...] = outs[0]


def short_convs(features, rim_rows, filters, usable):
    _, tok_dev, width_here = features.shape
    tile = min(CONV_TILE, width_here)
    return pl.pallas_call(
        conv_kernel,
        grid=(width_here // tile,),
        in_specs=[
            pl.BlockSpec((3, tok_dev, tile), lambda i: (0, 0, i)),
            pl.BlockSpec((3, SHORT - 1, tile), lambda i: (0, 0, i)),
            pl.BlockSpec((3, SHORT, tile), lambda i: (0, 0, i)),
            pl.BlockSpec((SHORT, tok_dev, 1), lambda i: (0, 0, 0)),
        ],
        out_specs=[
            pl.BlockSpec((tok_dev, tile), lambda i: (0, i)),
            pl.BlockSpec((tok_dev, tile), lambda i: (0, i)),
        ],
        out_shape=[
            jax.ShapeDtypeStruct((tok_dev, width_here), jnp.bfloat16),
            jax.ShapeDtypeStruct((tok_dev, width_here), jnp.float32),
        ],
    )(features, rim_rows, filters, usable)


def from_behind(shard, axis, by):
    length = lax.axis_size(axis)
    pairs = [(i, i + by) for i in range(length) if 0 <= i + by < length]
    return lax.ppermute(shard, axis, pairs)


def from_behind_2(value, axis, steps):
    count = lax.axis_size(axis)
    pairs = [(source, (source + steps) % count) for source in range(count)]
    return lax.ppermute(value, axis, pairs)


def butterfly_sum(value, axis):
    count = lax.axis_size(axis)
    step = 1
    while step < count:
        pairs = [(i, i ^ step) for i in range(count)]
        value = value + lax.ppermute(value, axis, pairs)
        step *= 2
    return value


def segment_starts(seq_lengths, positions):
    count = seq_lengths.shape[0]
    before = jnp.arange(count)[:, None] < jnp.arange(count)[None, :]
    starts = jnp.sum(jnp.where(before, seq_lengths[:, None], 0), axis=0)
    chosen = jnp.where(starts[None, :] <= positions[:, None], starts[None, :], 0)
    return jnp.max(chosen, axis=1)


def prior_states(fresh, pole_rate, keep, block_len):
    ctx_count = lax.axis_size("ctx")
    need = min(ctx_count, LONGEST // block_len + 1)
    groups, modes, lanes = fresh.shape
    ctx_pos = lax.axis_index("ctx")
    blocks = jnp.arange(ctx_count, dtype=jnp.int32)

    covers = []
    cover = 1
    while True:
        covers.append(cover)
        if 2 * cover - 1 >= need:
            break
        cover *= 2
    spans = []
    for cover in covers:
        spans.append((1 - cover, -1, cover - 1))
        spans.append((1 - cover, 0, cover))
    first = jnp.array([sp[0] for sp in spans], jnp.int32) + ctx_pos
    last = jnp.array([sp[1] for sp in spans], jnp.int32) + ctx_pos
    length = jnp.array([float(sp[2] * block_len) for sp in spans], jnp.float32)
    inside = (blocks[None, :] >= first[:, None]) & (blocks[None, :] <= last[:, None])
    whole = jnp.min(jnp.where(inside, keep.astype(jnp.float32)[None, :], 1.0), axis=1)
    decays = whole[:, None, None] * jnp.exp(-pole_rate[None] * length[:, None, None])

    inc_state = fresh
    exc_state = jnp.zeros_like(fresh)
    for index, cover in enumerate(covers):
        sent = inc_state.reshape(groups * modes, lanes).astype(jnp.bfloat16)
        got = from_behind(sent, "ctx", cover).astype(jnp.float32)
        got = got.reshape(groups, modes, lanes)
        exc_decay = decays[2 * index]
        if index == len(covers) - 1:
            return exc_decay, exc_state, got
        exc_state = exc_decay[..., None] * got + exc_state
        inc_state = decays[2 * index + 1][..., None] * got + inc_state


def ring_sum(value, axis):
    count = lax.axis_size(axis)
    total = value
    for shift in range(1, count):
        pairs = [(i, (i + shift) % count) for i in range(count)]
        total = total + lax.ppermute(value, axis, pairs)
    return total


def block_diagonal(state):
    groups, modes, lanes = state.shape
    same = jnp.arange(groups)[:, None] == jnp.arange(groups)[None, :]
    spread = jnp.where(same[:, None, :, None], state[:, :, None, :], 0.0)
    return spread.reshape(groups * modes, groups * lanes)


def on_device(projected, short_filter, decay_rate, residue, norm_gain, lengths):
    features = projected[0]
    filters = short_filter[0]
    pole_rate = decay_rate[0]
    residue_here = residue[0]
    seq_lengths = lengths[0]
    tok_dev = features.shape[1]
    width_here = features.shape[2]
    group_count = width_here // GW
    modes = pole_rate.shape[1]
    full_width = width_here * lax.axis_size("chan")
    ctx_pos = lax.axis_index("ctx")
    anchor = ctx_pos * tok_dev
    within = jnp.arange(tok_dev, dtype=jnp.int32)
    positions = anchor + within
    starts = segment_starts(seq_lengths, positions)

    rim_rows = from_behind(features[:, tok_dev - (SHORT - 1) :, :], "ctx", 1)
    usable = jnp.stack(
        [(positions - tap_index >= starts).astype(jnp.float32) for tap_index in range(SHORT)]
    )[:, :, None]
    gated_prod, query_conv = short_convs(features, rim_rows, filters, usable)
    values = gated_prod.reshape(tok_dev, group_count, GW)

    last_start = starts[tok_dev - 1]
    kept_rows = (positions >= last_start).astype(jnp.float32)
    fading = (
        jnp.exp(-pole_rate[None] * (tok_dev - 1 - within)[:, None, None].astype(jnp.float32))
        * kept_rows[:, None, None]
    )
    fresh_state = jnp.einsum(
        "sgm,sgc->gmc", fading, values.astype(jnp.float32), precision=HIGHEST
    )
    ctx_count = lax.axis_size("ctx")
    block_first = jnp.arange(ctx_count, dtype=jnp.int32) * tok_dev
    keep = segment_starts(seq_lengths, block_first + tok_dev - 1) < block_first
    earlier_decay, earlier_state, last_state = prior_states(fresh_state, pole_rate, keep, tok_dev)

    middle = tok_dev // 2
    offsets = (within - middle).astype(jnp.float32)
    left = residue_here[:, None, :] * jnp.exp(-pole_rate[:, None, :] * offsets[None, :, None])
    right = jnp.exp(pole_rate[:, :, None] * offsets[None, None, :])
    summed = jnp.einsum("gtm,gms->gts", left, right, precision=HIGHEST)
    inside = (within[None, :] <= within[:, None]) & (positions[None, :] >= starts[:, None])
    masked = jnp.where(inside[None], summed, 0.0).astype(jnp.bfloat16)
    intra_term = jnp.einsum("gts,sgc->tgc", masked, values, preferred_element_type=jnp.float32)

    carry_rows = (starts < anchor).astype(jnp.float32)
    reaching = (
        residue_here[None]
        * jnp.exp(-pole_rate[None] * (within + 1)[:, None, None].astype(jnp.float32))
        * carry_rows[:, None, None]
    )
    flat_reach = reaching.reshape(tok_dev, group_count * modes)
    early_part = intra_term.reshape(tok_dev, width_here) + jnp.dot(
        flat_reach, block_diagonal(earlier_state), precision=HIGH
    )
    late_reach = (reaching * earlier_decay[None]).reshape(tok_dev, group_count * modes)
    inter_late = jnp.dot(late_reach, block_diagonal(last_state), precision=HIGH)
    mixed_conv = (early_part + inter_late).astype(jnp.bfloat16)

    activity = query_conv * mixed_conv.astype(jnp.float32)
    squares = lax.psum(jnp.sum(activity * activity, axis=1), "chan")
    normed = (
        activity * lax.rsqrt(squares[:, None] / full_width + EPSILON) * norm_gain[0][None, :]
    ).astype(jnp.bfloat16)
    handoff = from_behind_2(normed, "phase", 1)
    return handoff[None]


def solution(mesh):
    in_specs = (
        P("phase", None, "ctx", "chan"),
        P("phase", None, None, "chan"),
        P("phase", "chan", None),
        P("phase", "chan", None),
        P("phase", "chan"),
        P("phase", None),
    )
    out_specs = P("phase", "ctx", "chan")
    return jax.shard_map(
        on_device, mesh=mesh, in_specs=in_specs, out_specs=out_specs, check_vma=False
    )
```

```python
import jax
import jax.numpy as jnp
from jax import lax
from jax.sharding import PartitionSpec as P

GW = 128
SHORT = 3
LONGEST = 6144

EPSILON = 1e-05
HIGHEST = lax.Precision.HIGHEST
HIGH = lax.Precision.HIGH


def from_behind(shard, axis, by):
    length = lax.axis_size(axis)
    pairs = [(i, i + by) for i in range(length) if 0 <= i + by < length]
    return lax.ppermute(shard, axis, pairs)


def from_behind_2(value, axis, steps):
    count = lax.axis_size(axis)
    pairs = [(source, (source + steps) % count) for source in range(count)]
    return lax.ppermute(value, axis, pairs)


def butterfly_sum(value, axis):
    count = lax.axis_size(axis)
    step = 1
    while step < count:
        pairs = [(i, i ^ step) for i in range(count)]
        value = value + lax.ppermute(value, axis, pairs)
        step *= 2
    return value


def segment_starts(seq_lengths, positions):
    count = seq_lengths.shape[0]
    before = jnp.arange(count)[:, None] < jnp.arange(count)[None, :]
    starts = jnp.sum(jnp.where(before, seq_lengths[:, None], 0), axis=0)
    chosen = jnp.where(starts[None, :] <= positions[:, None], starts[None, :], 0)
    return jnp.max(chosen, axis=1)


def prior_states(fresh, pole_rate, keep, block_len):
    ctx_count = lax.axis_size("ctx")
    need = min(ctx_count, LONGEST // block_len + 1)
    groups, modes, lanes = fresh.shape
    ctx_pos = lax.axis_index("ctx")
    blocks = jnp.arange(ctx_count, dtype=jnp.int32)

    covers = []
    cover = 1
    while True:
        covers.append(cover)
        if 2 * cover - 1 >= need:
            break
        cover *= 2
    spans = []
    for cover in covers:
        spans.append((1 - cover, -1, cover - 1))
        spans.append((1 - cover, 0, cover))
    first = jnp.array([sp[0] for sp in spans], jnp.int32) + ctx_pos
    last = jnp.array([sp[1] for sp in spans], jnp.int32) + ctx_pos
    length = jnp.array([float(sp[2] * block_len) for sp in spans], jnp.float32)
    inside = (blocks[None, :] >= first[:, None]) & (blocks[None, :] <= last[:, None])
    whole = jnp.min(jnp.where(inside, keep.astype(jnp.float32)[None, :], 1.0), axis=1)
    decays = whole[:, None, None] * jnp.exp(-pole_rate[None] * length[:, None, None])

    inc_state = fresh
    exc_state = jnp.zeros_like(fresh)
    for index, cover in enumerate(covers):
        sent = inc_state.reshape(groups * modes, lanes).astype(jnp.bfloat16)
        got = from_behind(sent, "ctx", cover).astype(jnp.float32)
        got = got.reshape(groups, modes, lanes)
        exc_decay = decays[2 * index]
        if index == len(covers) - 1:
            return exc_decay, exc_state, got
        exc_state = exc_decay[..., None] * got + exc_state
        inc_state = decays[2 * index + 1][..., None] * got + inc_state


def ring_sum(value, axis):
    count = lax.axis_size(axis)
    total = value
    for shift in range(1, count):
        pairs = [(i, (i + shift) % count) for i in range(count)]
        total = total + lax.ppermute(value, axis, pairs)
    return total


def block_diagonal(state):
    groups, modes, lanes = state.shape
    same = jnp.arange(groups)[:, None] == jnp.arange(groups)[None, :]
    spread = jnp.where(same[:, None, :, None], state[:, :, None, :], 0.0)
    return spread.reshape(groups * modes, groups * lanes)


def on_device(projected, short_filter, decay_rate, residue, norm_gain, lengths):
    features = projected[0]
    filters = short_filter[0]
    pole_rate = decay_rate[0]
    residue_here = residue[0]
    seq_lengths = lengths[0]
    tok_dev = features.shape[1]
    width_here = features.shape[2]
    group_count = width_here // GW
    modes = pole_rate.shape[1]
    full_width = width_here * lax.axis_size("chan")
    ctx_pos = lax.axis_index("ctx")
    anchor = ctx_pos * tok_dev
    within = jnp.arange(tok_dev, dtype=jnp.int32)
    positions = anchor + within
    starts = segment_starts(seq_lengths, positions)

    rim_rows = from_behind(features[:, tok_dev - (SHORT - 1) :, :], "ctx", 1)
    extended = jnp.concatenate([rim_rows, features], axis=1)
    short_out = jnp.zeros((3, tok_dev, width_here), jnp.float32)
    for tap_index in range(SHORT):
        shifted = extended[:, SHORT - 1 - tap_index : SHORT - 1 - tap_index + tok_dev]
        usable = (positions - tap_index >= starts).astype(jnp.float32)
        short_out = (
            short_out
            + filters[:, tap_index, None, :] * shifted.astype(jnp.float32) * usable[None, :, None]
        )
    gated_prod = (short_out[1] * short_out[2]).astype(jnp.bfloat16)
    values = gated_prod.reshape(tok_dev, group_count, GW)

    last_start = starts[tok_dev - 1]
    kept_rows = (positions >= last_start).astype(jnp.float32)
    fading = (
        jnp.exp(-pole_rate[None] * (tok_dev - 1 - within)[:, None, None].astype(jnp.float32))
        * kept_rows[:, None, None]
    )
    fresh_state = jnp.einsum(
        "sgm,sgc->gmc", fading, values.astype(jnp.float32), precision=HIGH
    )
    ctx_count = lax.axis_size("ctx")
    block_first = jnp.arange(ctx_count, dtype=jnp.int32) * tok_dev
    keep = segment_starts(seq_lengths, block_first + tok_dev - 1) < block_first
    earlier_decay, earlier_state, last_state = prior_states(fresh_state, pole_rate, keep, tok_dev)

    middle = tok_dev // 2
    offsets = (within - middle).astype(jnp.float32)
    left = residue_here[:, None, :] * jnp.exp(-pole_rate[:, None, :] * offsets[None, :, None])
    right = jnp.exp(pole_rate[:, :, None] * offsets[None, None, :])
    summed = jnp.einsum("gtm,gms->gts", left, right, precision=HIGH)
    inside = (within[None, :] <= within[:, None]) & (positions[None, :] >= starts[:, None])
    masked = jnp.where(inside[None], summed, 0.0).astype(jnp.bfloat16)
    intra_term = jnp.einsum("gts,sgc->tgc", masked, values, preferred_element_type=jnp.float32)

    carry_rows = (starts < anchor).astype(jnp.float32)
    reaching = (
        residue_here[None]
        * jnp.exp(-pole_rate[None] * (within + 1)[:, None, None].astype(jnp.float32))
        * carry_rows[:, None, None]
    )
    flat_reach = reaching.reshape(tok_dev, group_count * modes)
    early_part = intra_term.reshape(tok_dev, width_here) + jnp.dot(
        flat_reach, block_diagonal(earlier_state), precision=HIGH
    )
    late_reach = (reaching * earlier_decay[None]).reshape(tok_dev, group_count * modes)
    inter_late = jnp.dot(late_reach, block_diagonal(last_state), precision=HIGH)
    mixed_conv = (early_part + inter_late).astype(jnp.bfloat16)

    activity = short_out[0] * mixed_conv.astype(jnp.float32)
    squares = lax.psum(jnp.sum(activity * activity, axis=1), "chan")
    normed = (
        activity * lax.rsqrt(squares[:, None] / full_width + EPSILON) * norm_gain[0][None, :]
    ).astype(jnp.bfloat16)
    handoff = from_behind_2(normed, "phase", 1)
    return handoff[None]


def solution(mesh):
    in_specs = (
        P("phase", None, "ctx", "chan"),
        P("phase", None, None, "chan"),
        P("phase", "chan", None),
        P("phase", "chan", None),
        P("phase", "chan"),
        P("phase", None),
    )
    out_specs = P("phase", "ctx", "chan")
    return jax.shard_map(
        on_device, mesh=mesh, in_specs=in_specs, out_specs=out_specs, check_vma=False
    )
```

```python
import jax
import jax.numpy as jnp
from jax import lax
from jax.sharding import PartitionSpec as P

GW = 128
SHORT = 3
LONGEST = 6144

EPSILON = 1e-05
HIGHEST = lax.Precision.HIGHEST
HIGH = lax.Precision.HIGH


def from_behind(shard, axis, by):
    length = lax.axis_size(axis)
    pairs = [(i, i + by) for i in range(length) if 0 <= i + by < length]
    return lax.ppermute(shard, axis, pairs)


def from_behind_2(value, axis, steps):
    count = lax.axis_size(axis)
    pairs = [(source, (source + steps) % count) for source in range(count)]
    return lax.ppermute(value, axis, pairs)


def butterfly_sum(value, axis):
    count = lax.axis_size(axis)
    step = 1
    while step < count:
        pairs = [(i, i ^ step) for i in range(count)]
        value = value + lax.ppermute(value, axis, pairs)
        step *= 2
    return value


def segment_starts(seq_lengths, positions):
    count = seq_lengths.shape[0]
    before = jnp.arange(count)[:, None] < jnp.arange(count)[None, :]
    starts = jnp.sum(jnp.where(before, seq_lengths[:, None], 0), axis=0)
    chosen = jnp.where(starts[None, :] <= positions[:, None], starts[None, :], 0)
    return jnp.max(chosen, axis=1)


def prior_states(fresh, pole_rate, keep, block_len):
    ctx_count = lax.axis_size("ctx")
    need = min(ctx_count, LONGEST // block_len + 1)
    groups, modes, lanes = fresh.shape
    ctx_pos = lax.axis_index("ctx")
    blocks = jnp.arange(ctx_count, dtype=jnp.int32)

    covers = []
    cover = 1
    while True:
        covers.append(cover)
        if 2 * cover - 1 >= need:
            break
        cover *= 2
    spans = []
    for cover in covers:
        spans.append((1 - cover, -1, cover - 1))
        spans.append((1 - cover, 0, cover))
    first = jnp.array([sp[0] for sp in spans], jnp.int32) + ctx_pos
    last = jnp.array([sp[1] for sp in spans], jnp.int32) + ctx_pos
    length = jnp.array([float(sp[2] * block_len) for sp in spans], jnp.float32)
    inside = (blocks[None, :] >= first[:, None]) & (blocks[None, :] <= last[:, None])
    whole = jnp.min(jnp.where(inside, keep.astype(jnp.float32)[None, :], 1.0), axis=1)
    decays = whole[:, None, None] * jnp.exp(-pole_rate[None] * length[:, None, None])

    inc_state = fresh
    exc_state = jnp.zeros_like(fresh)
    for index, cover in enumerate(covers):
        sent = inc_state.reshape(groups * modes, lanes).astype(jnp.bfloat16)
        got = from_behind(sent, "ctx", cover).astype(jnp.float32)
        got = got.reshape(groups, modes, lanes)
        exc_decay = decays[2 * index]
        if index == len(covers) - 1:
            return exc_decay, exc_state, got
        exc_state = exc_decay[..., None] * got + exc_state
        inc_state = decays[2 * index + 1][..., None] * got + inc_state


def ring_sum(value, axis):
    count = lax.axis_size(axis)
    total = value
    for shift in range(1, count):
        pairs = [(i, (i + shift) % count) for i in range(count)]
        total = total + lax.ppermute(value, axis, pairs)
    return total


def block_diagonal(state):
    groups, modes, lanes = state.shape
    same = jnp.arange(groups)[:, None] == jnp.arange(groups)[None, :]
    spread = jnp.where(same[:, None, :, None], state[:, :, None, :], 0.0)
    return spread.reshape(groups * modes, groups * lanes)


def on_device(projected, short_filter, decay_rate, residue, norm_gain, lengths):
    features = projected[0]
    filters = short_filter[0]
    pole_rate = decay_rate[0]
    residue_here = residue[0]
    seq_lengths = lengths[0]
    tok_dev = features.shape[1]
    width_here = features.shape[2]
    group_count = width_here // GW
    modes = pole_rate.shape[1]
    full_width = width_here * lax.axis_size("chan")
    ctx_pos = lax.axis_index("ctx")
    anchor = ctx_pos * tok_dev
    within = jnp.arange(tok_dev, dtype=jnp.int32)
    positions = anchor + within
    starts = segment_starts(seq_lengths, positions)

    rim_rows = from_behind(features[:, tok_dev - (SHORT - 1) :, :], "ctx", 1)
    extended = jnp.concatenate([rim_rows, features], axis=1)
    short_out = jnp.zeros((3, tok_dev, width_here), jnp.float32)
    for tap_index in range(SHORT):
        shifted = extended[:, SHORT - 1 - tap_index : SHORT - 1 - tap_index + tok_dev]
        usable = (positions - tap_index >= starts).astype(jnp.float32)
        short_out = (
            short_out
            + filters[:, tap_index, None, :] * shifted.astype(jnp.float32) * usable[None, :, None]
        )
    gated_prod = (short_out[1] * short_out[2]).astype(jnp.bfloat16)
    values = gated_prod.reshape(tok_dev, group_count, GW)

    last_start = starts[tok_dev - 1]
    kept_rows = (positions >= last_start).astype(jnp.float32)
    fading = (
        jnp.exp(-pole_rate[None] * (tok_dev - 1 - within)[:, None, None].astype(jnp.float32))
        * kept_rows[:, None, None]
    )
    fresh_state = jnp.einsum(
        "sgm,sgc->gmc", fading, values.astype(jnp.float32), precision=HIGH
    )
    ctx_count = lax.axis_size("ctx")
    block_first = jnp.arange(ctx_count, dtype=jnp.int32) * tok_dev
    keep = segment_starts(seq_lengths, block_first + tok_dev - 1) < block_first
    aligned = lax.psum(features[0, 0, :GW].astype(jnp.float32), ("ctx", "chan", "phase"))
    fresh_state = fresh_state + 0.0 * aligned[None, None, :]
    earlier_decay, earlier_state, last_state = prior_states(fresh_state, pole_rate, keep, tok_dev)

    middle = tok_dev // 2
    offsets = (within - middle).astype(jnp.float32)
    left = residue_here[:, None, :] * jnp.exp(-pole_rate[:, None, :] * offsets[None, :, None])
    right = jnp.exp(pole_rate[:, :, None] * offsets[None, None, :])
    summed = jnp.einsum("gtm,gms->gts", left, right, precision=HIGH)
    inside = (within[None, :] <= within[:, None]) & (positions[None, :] >= starts[:, None])
    masked = jnp.where(inside[None], summed, 0.0).astype(jnp.bfloat16)
    intra_term = jnp.einsum("gts,sgc->tgc", masked, values, preferred_element_type=jnp.float32)

    carry_rows = (starts < anchor).astype(jnp.float32)
    reaching = (
        residue_here[None]
        * jnp.exp(-pole_rate[None] * (within + 1)[:, None, None].astype(jnp.float32))
        * carry_rows[:, None, None]
    )
    flat_reach = reaching.reshape(tok_dev, group_count * modes)
    early_part = intra_term.reshape(tok_dev, width_here) + jnp.dot(
        flat_reach, block_diagonal(earlier_state), precision=HIGH
    )
    late_reach = (reaching * earlier_decay[None]).reshape(tok_dev, group_count * modes)
    inter_late = jnp.dot(late_reach, block_diagonal(last_state), precision=HIGH)
    mixed_conv = (early_part + inter_late).astype(jnp.bfloat16)

    activity = short_out[0] * mixed_conv.astype(jnp.float32)
    squares = lax.psum(jnp.sum(activity * activity, axis=1), "chan")
    normed = (
        activity * lax.rsqrt(squares[:, None] / full_width + EPSILON) * norm_gain[0][None, :]
    ).astype(jnp.bfloat16)
    handoff = from_behind_2(normed, "phase", 1)
    return handoff[None]


def solution(mesh):
    in_specs = (
        P("phase", None, "ctx", "chan"),
        P("phase", None, None, "chan"),
        P("phase", "chan", None),
        P("phase", "chan", None),
        P("phase", "chan"),
        P("phase", None),
    )
    out_specs = P("phase", "ctx", "chan")
    return jax.shard_map(
        on_device, mesh=mesh, in_specs=in_specs, out_specs=out_specs, check_vma=False
    )
```

```python
import jax
import jax.numpy as jnp
from jax import lax
from jax.sharding import PartitionSpec as P

GW = 128
SHORT = 3
LONGEST = 6144

EPSILON = 1e-05
HIGHEST = lax.Precision.HIGHEST
HIGH = lax.Precision.HIGH


def from_behind(shard, axis, by):
    length = lax.axis_size(axis)
    pairs = [(i, i + by) for i in range(length) if 0 <= i + by < length]
    return lax.ppermute(shard, axis, pairs)


def from_behind_2(value, axis, steps):
    count = lax.axis_size(axis)
    pairs = [(source, (source + steps) % count) for source in range(count)]
    return lax.ppermute(value, axis, pairs)


def butterfly_sum(value, axis):
    count = lax.axis_size(axis)
    step = 1
    while step < count:
        pairs = [(i, i ^ step) for i in range(count)]
        value = value + lax.ppermute(value, axis, pairs)
        step *= 2
    return value


def segment_starts(seq_lengths, positions):
    count = seq_lengths.shape[0]
    before = jnp.arange(count)[:, None] < jnp.arange(count)[None, :]
    starts = jnp.sum(jnp.where(before, seq_lengths[:, None], 0), axis=0)
    chosen = jnp.where(starts[None, :] <= positions[:, None], starts[None, :], 0)
    return jnp.max(chosen, axis=1)


def prior_states(fresh, pole_rate, keep, block_len):
    ctx_count = lax.axis_size("ctx")
    need = min(ctx_count, LONGEST // block_len + 1)
    groups, modes, lanes = fresh.shape
    ctx_pos = lax.axis_index("ctx")
    blocks = jnp.arange(ctx_count, dtype=jnp.int32)

    covers = []
    cover = 1
    while True:
        covers.append(cover)
        if 2 * cover - 1 >= need:
            break
        cover *= 2
    spans = []
    for cover in covers:
        spans.append((1 - cover, -1, cover - 1))
        spans.append((1 - cover, 0, cover))
    first = jnp.array([sp[0] for sp in spans], jnp.int32) + ctx_pos
    last = jnp.array([sp[1] for sp in spans], jnp.int32) + ctx_pos
    length = jnp.array([float(sp[2] * block_len) for sp in spans], jnp.float32)
    inside = (blocks[None, :] >= first[:, None]) & (blocks[None, :] <= last[:, None])
    whole = jnp.min(jnp.where(inside, keep.astype(jnp.float32)[None, :], 1.0), axis=1)
    decays = whole[:, None, None] * jnp.exp(-pole_rate[None] * length[:, None, None])

    inc_state = fresh
    exc_state = jnp.zeros_like(fresh)
    for index, cover in enumerate(covers):
        sent = inc_state.reshape(groups * modes, lanes).astype(jnp.bfloat16)
        got = from_behind(sent, "ctx", cover).astype(jnp.float32)
        got = got.reshape(groups, modes, lanes)
        exc_decay = decays[2 * index]
        if index == len(covers) - 1:
            return exc_decay, exc_state, got
        exc_state = exc_decay[..., None] * got + exc_state
        inc_state = decays[2 * index + 1][..., None] * got + inc_state


def ring_sum(value, axis):
    count = lax.axis_size(axis)
    total = value
    for shift in range(1, count):
        pairs = [(i, (i + shift) % count) for i in range(count)]
        total = total + lax.ppermute(value, axis, pairs)
    return total


def block_diagonal(state):
    groups, modes, lanes = state.shape
    same = jnp.arange(groups)[:, None] == jnp.arange(groups)[None, :]
    spread = jnp.where(same[:, None, :, None], state[:, :, None, :], 0.0)
    return spread.reshape(groups * modes, groups * lanes)


def on_device(projected, short_filter, decay_rate, residue, norm_gain, lengths):
    features = projected[0]
    filters = short_filter[0]
    pole_rate = decay_rate[0]
    residue_here = residue[0]
    seq_lengths = lengths[0]
    tok_dev = features.shape[1]
    width_here = features.shape[2]
    group_count = width_here // GW
    modes = pole_rate.shape[1]
    full_width = width_here * lax.axis_size("chan")
    ctx_pos = lax.axis_index("ctx")
    anchor = ctx_pos * tok_dev
    within = jnp.arange(tok_dev, dtype=jnp.int32)
    positions = anchor + within
    starts = segment_starts(seq_lengths, positions)

    rim_rows = from_behind(features[:, tok_dev - (SHORT - 1) :, :], "ctx", 1)
    extended = jnp.concatenate([rim_rows, features], axis=1)
    short_out = jnp.zeros((3, tok_dev, width_here), jnp.float32)
    for tap_index in range(SHORT):
        shifted = extended[:, SHORT - 1 - tap_index : SHORT - 1 - tap_index + tok_dev]
        usable = (positions - tap_index >= starts).astype(jnp.float32)
        short_out = (
            short_out
            + filters[:, tap_index, None, :] * shifted.astype(jnp.float32) * usable[None, :, None]
        )
    gated_prod = (short_out[1] * short_out[2]).astype(jnp.bfloat16)
    values = gated_prod.reshape(tok_dev, group_count, GW)

    last_start = starts[tok_dev - 1]
    kept_rows = (positions >= last_start).astype(jnp.float32)
    fading = (
        jnp.exp(-pole_rate[None] * (tok_dev - 1 - within)[:, None, None].astype(jnp.float32))
        * kept_rows[:, None, None]
    )
    fresh_state = jnp.einsum(
        "sgm,sgc->gmc", fading, values.astype(jnp.float32), precision=HIGH
    )
    ctx_count = lax.axis_size("ctx")
    block_first = jnp.arange(ctx_count, dtype=jnp.int32) * tok_dev
    keep = segment_starts(seq_lengths, block_first + tok_dev - 1) < block_first
    earlier_decay, earlier_state, last_state = prior_states(fresh_state, pole_rate, keep, tok_dev)

    middle = tok_dev // 2
    offsets = (within - middle).astype(jnp.float32)
    left = residue_here[:, None, :] * jnp.exp(-pole_rate[:, None, :] * offsets[None, :, None])
    right = jnp.exp(pole_rate[:, :, None] * offsets[None, None, :])
    summed = jnp.einsum("gtm,gms->gts", left, right, precision=HIGH)
    inside = (within[None, :] <= within[:, None]) & (positions[None, :] >= starts[:, None])
    masked = jnp.where(inside[None], summed, 0.0).astype(jnp.bfloat16)
    intra_term = jnp.einsum("gts,sgc->tgc", masked, values, preferred_element_type=jnp.float32)

    carry_rows = (starts < anchor).astype(jnp.float32)
    reaching = (
        residue_here[None]
        * jnp.exp(-pole_rate[None] * (within + 1)[:, None, None].astype(jnp.float32))
        * carry_rows[:, None, None]
    )
    flat_reach = reaching.reshape(tok_dev, group_count * modes)
    early_part = intra_term.reshape(tok_dev, width_here) + jnp.dot(
        flat_reach, block_diagonal(earlier_state), precision=HIGH
    )
    late_reach = (reaching * earlier_decay[None]).reshape(tok_dev, group_count * modes)
    inter_late = jnp.dot(late_reach, block_diagonal(last_state), precision=HIGH)
    mixed_conv = (early_part + inter_late).astype(jnp.bfloat16)

    activity = short_out[0] * mixed_conv.astype(jnp.float32)
    partial = jnp.sum(activity * activity, axis=1)
    chan_count = lax.axis_size("chan")
    spread = jnp.broadcast_to(partial[None], (chan_count,) + partial.shape)
    squares = jnp.sum(lax.all_to_all(spread, "chan", 0, 0, tiled=True), axis=0)
    normed = (
        activity * lax.rsqrt(squares[:, None] / full_width + EPSILON) * norm_gain[0][None, :]
    ).astype(jnp.bfloat16)
    handoff = from_behind_2(normed, "phase", 1)
    return handoff[None]


def solution(mesh):
    in_specs = (
        P("phase", None, "ctx", "chan"),
        P("phase", None, None, "chan"),
        P("phase", "chan", None),
        P("phase", "chan", None),
        P("phase", "chan"),
        P("phase", None),
    )
    out_specs = P("phase", "ctx", "chan")
    return jax.shard_map(
        on_device, mesh=mesh, in_specs=in_specs, out_specs=out_specs, check_vma=False
    )
```

```python
import jax
import jax.numpy as jnp
from jax import lax
from jax.sharding import PartitionSpec as P
from jax.experimental import pallas as pl
from jax.experimental.pallas import tpu as pltpu

GW = 128
SHORT = 3
LONGEST = 6144

EPSILON = 1e-05
HIGHEST = lax.Precision.HIGHEST
HIGH = lax.Precision.HIGH


CONV_TILE = 512


def conv_kernel(feat_ref, rim_ref, filt_ref, use_ref, gated_ref, query_ref):
    tok_dev, tile = gated_ref.shape
    rows = lax.broadcasted_iota(jnp.int32, (tok_dev, tile), 0)
    outs = []
    for which in range(3):
        plain = feat_ref[which].astype(jnp.float32)
        rim = rim_ref[which].astype(jnp.float32)
        total = jnp.zeros((tok_dev, tile), jnp.float32)
        for tap_index in range(SHORT):
            shifted = plain
            if tap_index:
                shifted = pltpu.roll(plain, tap_index, 0)
                for row in range(tap_index):
                    shifted = jnp.where(
                        rows == row, rim[SHORT - 1 - tap_index + row][None, :], shifted
                    )
            total = total + filt_ref[which, tap_index][None, :] * shifted * use_ref[tap_index]
        outs.append(total)
    gated_ref[...] = (outs[1] * outs[2]).astype(jnp.bfloat16)
    query_ref[...] = outs[0]


def short_convs(features, rim_rows, filters, usable):
    _, tok_dev, width_here = features.shape
    tile = min(CONV_TILE, width_here)
    return pl.pallas_call(
        conv_kernel,
        grid=(width_here // tile,),
        in_specs=[
            pl.BlockSpec((3, tok_dev, tile), lambda i: (0, 0, i)),
            pl.BlockSpec((3, SHORT - 1, tile), lambda i: (0, 0, i)),
            pl.BlockSpec((3, SHORT, tile), lambda i: (0, 0, i)),
            pl.BlockSpec((SHORT, tok_dev, 1), lambda i: (0, 0, 0)),
        ],
        out_specs=[
            pl.BlockSpec((tok_dev, tile), lambda i: (0, i)),
            pl.BlockSpec((tok_dev, tile), lambda i: (0, i)),
        ],
        out_shape=[
            jax.ShapeDtypeStruct((tok_dev, width_here), jnp.bfloat16),
            jax.ShapeDtypeStruct((tok_dev, width_here), jnp.float32),
        ],
    )(features, rim_rows, filters, usable)


def from_behind(shard, axis, by):
    length = lax.axis_size(axis)
    pairs = [(i, i + by) for i in range(length) if 0 <= i + by < length]
    return lax.ppermute(shard, axis, pairs)


def from_behind_2(value, axis, steps):
    count = lax.axis_size(axis)
    pairs = [(source, (source + steps) % count) for source in range(count)]
    return lax.ppermute(value, axis, pairs)


def butterfly_sum(value, axis):
    count = lax.axis_size(axis)
    step = 1
    while step < count:
        pairs = [(i, i ^ step) for i in range(count)]
        value = value + lax.ppermute(value, axis, pairs)
        step *= 2
    return value


def segment_starts(seq_lengths, positions):
    count = seq_lengths.shape[0]
    before = jnp.arange(count)[:, None] < jnp.arange(count)[None, :]
    starts = jnp.sum(jnp.where(before, seq_lengths[:, None], 0), axis=0)
    chosen = jnp.where(starts[None, :] <= positions[:, None], starts[None, :], 0)
    return jnp.max(chosen, axis=1)


def prior_states(fresh, pole_rate, keep, block_len):
    ctx_count = lax.axis_size("ctx")
    need = min(ctx_count, LONGEST // block_len + 1)
    groups, modes, lanes = fresh.shape
    ctx_pos = lax.axis_index("ctx")
    blocks = jnp.arange(ctx_count, dtype=jnp.int32)

    covers = []
    cover = 1
    while True:
        covers.append(cover)
        if 2 * cover - 1 >= need:
            break
        cover *= 2
    spans = []
    for cover in covers:
        spans.append((1 - cover, -1, cover - 1))
        spans.append((1 - cover, 0, cover))
    first = jnp.array([sp[0] for sp in spans], jnp.int32) + ctx_pos
    last = jnp.array([sp[1] for sp in spans], jnp.int32) + ctx_pos
    length = jnp.array([float(sp[2] * block_len) for sp in spans], jnp.float32)
    inside = (blocks[None, :] >= first[:, None]) & (blocks[None, :] <= last[:, None])
    whole = jnp.min(jnp.where(inside, keep.astype(jnp.float32)[None, :], 1.0), axis=1)
    decays = whole[:, None, None] * jnp.exp(-pole_rate[None] * length[:, None, None])

    inc_state = fresh
    exc_state = jnp.zeros_like(fresh)
    for index, cover in enumerate(covers):
        sent = inc_state.reshape(groups * modes, lanes).astype(jnp.bfloat16)
        got = from_behind(sent, "ctx", cover).astype(jnp.float32)
        got = got.reshape(groups, modes, lanes)
        exc_decay = decays[2 * index]
        if index == len(covers) - 1:
            return exc_decay, exc_state, got
        exc_state = exc_decay[..., None] * got + exc_state
        inc_state = decays[2 * index + 1][..., None] * got + inc_state


def ring_sum(value, axis):
    count = lax.axis_size(axis)
    total = value
    for shift in range(1, count):
        pairs = [(i, (i + shift) % count) for i in range(count)]
        total = total + lax.ppermute(value, axis, pairs)
    return total


def block_diagonal(state):
    groups, modes, lanes = state.shape
    same = jnp.arange(groups)[:, None] == jnp.arange(groups)[None, :]
    spread = jnp.where(same[:, None, :, None], state[:, :, None, :], 0.0)
    return spread.reshape(groups * modes, groups * lanes)


def on_device(projected, short_filter, decay_rate, residue, norm_gain, lengths):
    features = projected[0]
    filters = short_filter[0]
    pole_rate = decay_rate[0]
    residue_here = residue[0]
    seq_lengths = lengths[0]
    tok_dev = features.shape[1]
    width_here = features.shape[2]
    group_count = width_here // GW
    modes = pole_rate.shape[1]
    full_width = width_here * lax.axis_size("chan")
    ctx_pos = lax.axis_index("ctx")
    anchor = ctx_pos * tok_dev
    within = jnp.arange(tok_dev, dtype=jnp.int32)
    positions = anchor + within
    starts = segment_starts(seq_lengths, positions)

    rim_rows = from_behind(features[:, tok_dev - (SHORT - 1) :, :], "ctx", 1)
    usable = jnp.stack(
        [(positions - tap_index >= starts).astype(jnp.float32) for tap_index in range(SHORT)]
    )[:, :, None]
    gated_prod, query_conv = short_convs(features, rim_rows, filters, usable)
    values = gated_prod.reshape(tok_dev, group_count, GW)

    last_start = starts[tok_dev - 1]
    kept_rows = (positions >= last_start).astype(jnp.float32)
    fading = (
        jnp.exp(-pole_rate[None] * (tok_dev - 1 - within)[:, None, None].astype(jnp.float32))
        * kept_rows[:, None, None]
    )
    fresh_state = jnp.einsum(
        "sgm,sgc->gmc", fading, values.astype(jnp.float32), precision=HIGH
    )
    ctx_count = lax.axis_size("ctx")
    block_first = jnp.arange(ctx_count, dtype=jnp.int32) * tok_dev
    keep = segment_starts(seq_lengths, block_first + tok_dev - 1) < block_first
    earlier_decay, earlier_state, last_state = prior_states(fresh_state, pole_rate, keep, tok_dev)

    middle = tok_dev // 2
    offsets = (within - middle).astype(jnp.float32)
    left = residue_here[:, None, :] * jnp.exp(-pole_rate[:, None, :] * offsets[None, :, None])
    right = jnp.exp(pole_rate[:, :, None] * offsets[None, None, :])
    summed = jnp.einsum("gtm,gms->gts", left, right, precision=HIGH)
    inside = (within[None, :] <= within[:, None]) & (positions[None, :] >= starts[:, None])
    masked = jnp.where(inside[None], summed, 0.0).astype(jnp.bfloat16)
    intra_term = jnp.einsum("gts,sgc->tgc", masked, values, preferred_element_type=jnp.float32)

    carry_rows = (starts < anchor).astype(jnp.float32)
    reaching = (
        residue_here[None]
        * jnp.exp(-pole_rate[None] * (within + 1)[:, None, None].astype(jnp.float32))
        * carry_rows[:, None, None]
    )
    flat_reach = reaching.reshape(tok_dev, group_count * modes)
    early_part = intra_term.reshape(tok_dev, width_here) + jnp.dot(
        flat_reach, block_diagonal(earlier_state), precision=HIGH
    )
    late_reach = (reaching * earlier_decay[None]).reshape(tok_dev, group_count * modes)
    inter_late = jnp.dot(late_reach, block_diagonal(last_state), precision=HIGH)
    mixed_conv = (early_part + inter_late).astype(jnp.bfloat16)

    activity = query_conv * mixed_conv.astype(jnp.float32)
    partial = jnp.sum(activity * activity, axis=1)
    chan_count = lax.axis_size("chan")
    spread = jnp.broadcast_to(partial[None], (chan_count,) + partial.shape)
    squares = jnp.sum(lax.all_to_all(spread, "chan", 0, 0, tiled=True), axis=0)
    normed = (
        activity * lax.rsqrt(squares[:, None] / full_width + EPSILON) * norm_gain[0][None, :]
    ).astype(jnp.bfloat16)
    handoff = from_behind_2(normed, "phase", 1)
    return handoff[None]


def solution(mesh):
    in_specs = (
        P("phase", None, "ctx", "chan"),
        P("phase", None, None, "chan"),
        P("phase", "chan", None),
        P("phase", "chan", None),
        P("phase", "chan"),
        P("phase", None),
    )
    out_specs = P("phase", "ctx", "chan")
    return jax.shard_map(
        on_device, mesh=mesh, in_specs=in_specs, out_specs=out_specs, check_vma=False
    )
```

```python
import jax
import jax.numpy as jnp
from jax import lax
from jax.sharding import PartitionSpec as P

GW = 128
SHORT = 3
LONGEST = 6144

EPSILON = 1e-05
HIGHEST = lax.Precision.HIGHEST
HIGH = lax.Precision.HIGH


def from_behind(shard, axis, by):
    length = lax.axis_size(axis)
    pairs = [(i, i + by) for i in range(length) if 0 <= i + by < length]
    return lax.ppermute(shard, axis, pairs)


def from_behind_2(value, axis, steps):
    count = lax.axis_size(axis)
    pairs = [(source, (source + steps) % count) for source in range(count)]
    return lax.ppermute(value, axis, pairs)


def butterfly_sum(value, axis):
    count = lax.axis_size(axis)
    step = 1
    while step < count:
        pairs = [(i, i ^ step) for i in range(count)]
        value = value + lax.ppermute(value, axis, pairs)
        step *= 2
    return value


def segment_starts(seq_lengths, positions):
    count = seq_lengths.shape[0]
    before = jnp.arange(count)[:, None] < jnp.arange(count)[None, :]
    starts = jnp.sum(jnp.where(before, seq_lengths[:, None], 0), axis=0)
    chosen = jnp.where(starts[None, :] <= positions[:, None], starts[None, :], 0)
    return jnp.max(chosen, axis=1)


def prior_states(fresh, pole_rate, keep, block_len):
    ctx_count = lax.axis_size("ctx")
    need = min(ctx_count, LONGEST // block_len + 1)
    groups, modes, lanes = fresh.shape
    ctx_pos = lax.axis_index("ctx")
    blocks = jnp.arange(ctx_count, dtype=jnp.int32)

    covers = []
    cover = 1
    while True:
        covers.append(cover)
        if 2 * cover - 1 >= need:
            break
        cover *= 2
    spans = []
    for cover in covers:
        spans.append((1 - cover, -1, cover - 1))
        spans.append((1 - cover, 0, cover))
    first = jnp.array([sp[0] for sp in spans], jnp.int32) + ctx_pos
    last = jnp.array([sp[1] for sp in spans], jnp.int32) + ctx_pos
    length = jnp.array([float(sp[2] * block_len) for sp in spans], jnp.float32)
    inside = (blocks[None, :] >= first[:, None]) & (blocks[None, :] <= last[:, None])
    whole = jnp.min(jnp.where(inside, keep.astype(jnp.float32)[None, :], 1.0), axis=1)
    decays = whole[:, None, None] * jnp.exp(-pole_rate[None] * length[:, None, None])

    inc_state = fresh
    exc_state = jnp.zeros_like(fresh)
    for index, cover in enumerate(covers):
        sent = inc_state.reshape(groups * modes, lanes).astype(jnp.bfloat16)
        got = from_behind(sent, "ctx", cover).astype(jnp.float32)
        got = got.reshape(groups, modes, lanes)
        exc_decay = decays[2 * index]
        if index == len(covers) - 1:
            return exc_decay, exc_state, got
        exc_state = exc_decay[..., None] * got + exc_state
        inc_state = decays[2 * index + 1][..., None] * got + inc_state


def ring_sum(value, axis):
    count = lax.axis_size(axis)
    total = value
    for shift in range(1, count):
        pairs = [(i, (i + shift) % count) for i in range(count)]
        total = total + lax.ppermute(value, axis, pairs)
    return total


def block_diagonal(state):
    groups, modes, lanes = state.shape
    same = jnp.arange(groups)[:, None] == jnp.arange(groups)[None, :]
    spread = jnp.where(same[:, None, :, None], state[:, :, None, :], 0.0)
    return spread.reshape(groups * modes, groups * lanes)


def on_device(projected, short_filter, decay_rate, residue, norm_gain, lengths):
    features = projected[0]
    filters = short_filter[0]
    pole_rate = decay_rate[0]
    residue_here = residue[0]
    seq_lengths = lengths[0]
    tok_dev = features.shape[1]
    width_here = features.shape[2]
    group_count = width_here // GW
    modes = pole_rate.shape[1]
    full_width = width_here * lax.axis_size("chan")
    ctx_pos = lax.axis_index("ctx")
    anchor = ctx_pos * tok_dev
    within = jnp.arange(tok_dev, dtype=jnp.int32)
    positions = anchor + within
    starts = segment_starts(seq_lengths, positions)

    rim_rows = from_behind(features[:, tok_dev - (SHORT - 1) :, :], "ctx", 1)
    extended = jnp.concatenate([rim_rows, features], axis=1)
    short_out = jnp.zeros((3, tok_dev, width_here), jnp.float32)
    for tap_index in range(SHORT):
        shifted = extended[:, SHORT - 1 - tap_index : SHORT - 1 - tap_index + tok_dev]
        term = filters[:, tap_index, None, :] * shifted.astype(jnp.float32)
        if tap_index:
            usable = (positions - tap_index >= starts).astype(jnp.float32)
            term = term * usable[None, :, None]
        short_out = short_out + term
    gated_prod = (short_out[1] * short_out[2]).astype(jnp.bfloat16)
    values = gated_prod.reshape(tok_dev, group_count, GW)

    last_start = starts[tok_dev - 1]
    kept_rows = (positions >= last_start).astype(jnp.float32)
    fading = (
        jnp.exp(-pole_rate[None] * (tok_dev - 1 - within)[:, None, None].astype(jnp.float32))
        * kept_rows[:, None, None]
    )
    fresh_state = jnp.einsum(
        "sgm,sgc->gmc", fading, values.astype(jnp.float32), precision=HIGH
    )
    ctx_count = lax.axis_size("ctx")
    block_first = jnp.arange(ctx_count, dtype=jnp.int32) * tok_dev
    keep = segment_starts(seq_lengths, block_first + tok_dev - 1) < block_first
    earlier_decay, earlier_state, last_state = prior_states(fresh_state, pole_rate, keep, tok_dev)

    middle = tok_dev // 2
    offsets = (within - middle).astype(jnp.float32)
    left = residue_here[:, None, :] * jnp.exp(-pole_rate[:, None, :] * offsets[None, :, None])
    right = jnp.exp(pole_rate[:, :, None] * offsets[None, None, :])
    summed = jnp.einsum("gtm,gms->gts", left, right, precision=HIGH)
    inside = (within[None, :] <= within[:, None]) & (positions[None, :] >= starts[:, None])
    masked = jnp.where(inside[None], summed, 0.0).astype(jnp.bfloat16)
    intra_term = jnp.einsum("gts,sgc->tgc", masked, values, preferred_element_type=jnp.float32)

    carry_rows = (starts < anchor).astype(jnp.float32)
    reaching = (
        residue_here[None]
        * jnp.exp(-pole_rate[None] * (within + 1)[:, None, None].astype(jnp.float32))
        * carry_rows[:, None, None]
    )
    flat_reach = reaching.reshape(tok_dev, group_count * modes)
    early_part = intra_term.reshape(tok_dev, width_here) + jnp.dot(
        flat_reach, block_diagonal(earlier_state), precision=HIGH
    )
    late_reach = (reaching * earlier_decay[None]).reshape(tok_dev, group_count * modes)
    inter_late = jnp.dot(late_reach, block_diagonal(last_state), precision=HIGH)
    mixed_conv = (early_part + inter_late).astype(jnp.bfloat16)

    activity = short_out[0] * mixed_conv.astype(jnp.float32)
    partial = jnp.sum(activity * activity, axis=1)
    chan_count = lax.axis_size("chan")
    spread = jnp.broadcast_to(partial[None], (chan_count,) + partial.shape)
    squares = jnp.sum(lax.all_to_all(spread, "chan", 0, 0, tiled=True), axis=0)
    normed = (
        activity * lax.rsqrt(squares[:, None] / full_width + EPSILON) * norm_gain[0][None, :]
    ).astype(jnp.bfloat16)
    handoff = from_behind_2(normed, "phase", 1)
    return handoff[None]


def solution(mesh):
    in_specs = (
        P("phase", None, "ctx", "chan"),
        P("phase", None, None, "chan"),
        P("phase", "chan", None),
        P("phase", "chan", None),
        P("phase", "chan"),
        P("phase", None),
    )
    out_specs = P("phase", "ctx", "chan")
    return jax.shard_map(
        on_device, mesh=mesh, in_specs=in_specs, out_specs=out_specs, check_vma=False
    )
```
